512 devices in a mesh: seq: 64 (over z, x, y_lo), tensor: 8 (over y_hi, core).
Axes of the slice: x: 4, y: 8 (y_hi: 4, y_lo: 2; y = y_hi * 2 + y_lo), z: 8, core: 2. Of those that a mesh axis runs over, the one named last changes fastest.
Arguments:
- hidden_in: bfloat16 [8192, 2560], P('seq', 'tensor'), may hold values from -6 to 6
- norm_gain: float32 [2560], replicated, may hold values from 0.1 to 1.9
- w_query: bfloat16 [2560, 2048], P(None, 'tensor'), may hold values from -0.125 to 0.125
- w_key: bfloat16 [2560, 1024], P(None, 'tensor'), may hold values from -0.125 to 0.125
- w_value: bfloat16 [2560, 1024], P(None, 'tensor'), may hold values from -0.125 to 0.125
- w_out: bfloat16 [2048, 2560], P('tensor'), may hold values from -0.125 to 0.125
- q_gain: float32 [128], replicated, may hold values from 0.1 to 1.9
- k_gain: float32 [128], replicated, may hold values from 0.1 to 1.9
- lengths: int32 [16], replicated, may hold values from 1 to 6144, 8192 in all
Outputs:
- attn_out: bfloat16 [8192, 2560], P(('seq', 'tensor'))
- key_cache: bfloat16 [8192, 1024], P('seq', 'tensor')
- value_cache: bfloat16 [8192, 1024], P('seq', 'tensor')
The draws below stay inside these ranges and needn't reach their ends.
Inputs may be any that keep to these rules, and one draw needn't show every extreme that they name: The lengths sum to 8192 and the largest is exactly 6144.
All inputs are finite; a program needn't handle non-finite values.
Results may differ from the reference program's by a relative error of at most 0.015.
Values may be sent and summed in bfloat16 or wider, within the bound.
No kernel may reach another device: no remote copies, remote signals or barrier semaphores. Data moves between devices by JAX's collectives and lax.ppermute only.
A program may use at most 64 MiB of HBM per device.

```python
import math
import jax
import jax.numpy as jnp
import numpy as np
from jax import lax

D = 2560
HD = 128
KVH = 8
QH = 16
NSEG = 16
TOKENS = 8192
MAXLEN = 6144


def steps_of(rng, shape, cuts, least, largest):
    factor_of = 1.0
    for axis_at, parts in cuts:
        steps = jax.random.uniform(jax.random.fold_in(jax.random.fold_in(rng, 6), axis_at), (parts,), jnp.float32, least / len(cuts), largest / len(cuts))
        factor_of = factor_of * jnp.repeat(jnp.exp(steps), shape[axis_at] // parts).reshape((-1,) + (1,) * (len(shape) - 1 - axis_at))
    return factor_of


def length_profile(number_of, total, reach, skew):
    loads = [(1 << 20) // math.isqrt(standing ** skew) + 1 for standing in range(2, number_of + 1)]
    surplus, given = total - reach - (number_of - 1), [1] * (number_of - 1)
    while surplus > 0:
        candidates = [i for i in range(number_of - 1) if given[i] < reach]
        pool, left = sum([loads[i] for i in candidates]), surplus
        for i in candidates:
            more = min(reach - given[i], max(1, left * loads[i] // pool), surplus)
            given[i] = given[i] + more
            surplus = surplus - more
    return np.array([reach] + given)


def uneven_parts(rng, amount, total, limit, slope):
    if amount == 2:
        one = jax.random.randint(rng, (), max(1, total - limit), min(limit, total - 1) + 1)
        return jnp.stack([one, total - one])
    sizes = jnp.asarray(length_profile(amount, total, limit, slope), jnp.int32)
    pairs = (amount - 1) // 2
    source_of, taker = sizes[1:1 + 2 * pairs:2], sizes[2:2 + 2 * pairs:2]
    margin = jnp.minimum(source_of - 1, limit - taker)
    passed = jax.random.randint(jax.random.fold_in(rng, 1), (pairs,), 0, 1 << 20) % (margin + 1)
    sizes = sizes.at[1:1 + 2 * pairs:2].set(source_of - passed).at[2:2 + 2 * pairs:2].set(taker + passed)
    return sizes[jax.random.permutation(jax.random.fold_in(rng, 2), amount)]


def bell_draw(key, extent, scale, bound, pieces=(), kind=jnp.bfloat16):
    drawn = jax.random.normal(key, extent, jnp.float32) * scale
    if len(pieces) > 0:
        drawn = steps_of(key, extent, pieces, -0.22, 0.18) * drawn
    return jnp.clip(drawn, min=-bound, max=bound).astype(kind)


def setup_inputs(seed: int = 0) -> dict:
    key_list = jax.random.split(jax.random.key(seed), 10)
    hidden_in = bell_draw(key_list[0], (TOKENS, D), 1.0, 6.0, ((0, 64), (1, 8)))
    norm_gain = jnp.clip(1.0 + 0.18 * jax.random.normal(key_list[1], (D,), jnp.float32), 0.1, 1.9)
    w_query = bell_draw(key_list[2], (D, QH * HD), D ** -0.5, 0.125, ((1, 8),))
    w_key = bell_draw(key_list[3], (D, KVH * HD), D ** -0.5, 0.125, ((1, 8),))
    w_value = bell_draw(key_list[4], (D, KVH * HD), D ** -0.5, 0.125, ((1, 8),))
    w_out = bell_draw(key_list[5], (QH * HD, D), (QH * HD) ** -0.5, 0.125, ((0, 8),))
    q_gain = jnp.clip(1.0 + 0.18 * jax.random.normal(key_list[6], (HD,), jnp.float32), 0.1, 1.9)
    k_gain = jnp.clip(1.0 + 0.18 * jax.random.normal(key_list[7], (HD,), jnp.float32), 0.1, 1.9)
    lengths = uneven_parts(key_list[8], NSEG, TOKENS, MAXLEN, 2).astype(jnp.int32)
    return {"hidden_in": hidden_in, "norm_gain": norm_gain, "w_query": w_query, "w_key": w_key, "w_value": w_value, "w_out": w_out, "q_gain": q_gain, "k_gain": k_gain, "lengths": lengths}


rope_base = 1000000.0
norm_eps = 1e-06
masked = -1e+30

def prompt_starts(lengths, token_pos):
    ends = jnp.cumsum(lengths)
    starts = ends - lengths
    before = (ends[None, :] <= token_pos[:, None]).astype(jnp.int32)
    segment = lax.optimization_barrier(jnp.sum(before, axis=1))
    onehot = segment[:, None] == jnp.arange(lengths.shape[0], dtype=jnp.int32)[None, :]
    return lax.optimization_barrier(jnp.sum(jnp.where(onehot, starts[None, :], 0), axis=1)).astype(jnp.int32)

def head_norm_rope(values, gain, rel_pos):
    width = values.shape[-1]
    half = width // 2
    mean_sq = lax.optimization_barrier(jnp.mean(values * values, axis=-1, keepdims=True))
    normed = values * lax.rsqrt(mean_sq + norm_eps) * gain
    freq = rope_base ** (-jnp.arange(half, dtype=jnp.float32) * 2.0 / width)
    angle = rel_pos.astype(jnp.float32)[:, None] * freq[None, :]
    cosine = jnp.cos(angle)[:, None, :]
    sine = jnp.sin(angle)[:, None, :]
    first = normed[..., :half]
    second = normed[..., half:]
    return jnp.concatenate([first * cosine - second * sine, second * cosine + first * sine], axis=-1)

def reference(hidden_in, norm_gain, w_query, w_key, w_value, w_out, q_gain, k_gain, lengths):
    count = hidden_in.shape[0]
    width = hidden_in.shape[1]
    head_dim = q_gain.shape[0]
    q_heads = w_query.shape[1] // head_dim
    kv_heads = w_key.shape[1] // head_dim
    group = q_heads // kv_heads
    token_pos = jnp.arange(count, dtype=jnp.int32)
    seg_start = prompt_starts(lengths, token_pos)
    rel_pos = token_pos - seg_start
    wide = hidden_in.astype(jnp.float32)
    scaled = (wide * norm_gain[None, :]).astype(jnp.bfloat16)
    inv_rms = lax.rsqrt(lax.optimization_barrier(jnp.sum(wide * wide, axis=1)) / width + norm_eps)[:, None]
    q_raw = jnp.dot(scaled, w_query, preferred_element_type=jnp.float32) * inv_rms
    k_raw = jnp.dot(scaled, w_key, preferred_element_type=jnp.float32) * inv_rms
    value_cache = (jnp.dot(scaled, w_value, preferred_element_type=jnp.float32) * inv_rms).astype(jnp.bfloat16)
    queries = head_norm_rope(q_raw.reshape(count, q_heads, head_dim), q_gain, rel_pos).astype(jnp.bfloat16)
    keys = head_norm_rope(k_raw.reshape(count, kv_heads, head_dim), k_gain, rel_pos).astype(jnp.bfloat16)
    key_cache = keys.reshape(count, kv_heads * head_dim)
    query_grid = jnp.transpose(queries.reshape(count, kv_heads, group, head_dim), (1, 0, 2, 3))
    key_grid = jnp.transpose(keys, (1, 0, 2))
    value_grid = jnp.transpose(value_cache.reshape(count, kv_heads, head_dim), (1, 0, 2))
    block = math.gcd(count, 512)
    blocks = count // block
    inv_root = 1.0 / math.sqrt(head_dim)

    def one_head(operands):
        q_head, k_head, v_head = operands
        k_wide = k_head.astype(jnp.float32)
        v_wide = v_head.astype(jnp.float32)

        def one_block(index):
            first = (index * block).astype(jnp.int32)
            q_block = lax.dynamic_slice_in_dim(q_head, first, block, 0).astype(jnp.float32)
            q_pos = first + jnp.arange(block, dtype=jnp.int32)
            q_start = lax.dynamic_slice_in_dim(seg_start, first, block, 0)
            score = jnp.einsum('qgd,kd->gqk', q_block, k_wide) * inv_root
            visible = (token_pos[None, :] >= q_start[:, None]) & (token_pos[None, :] <= q_pos[:, None])
            score = jnp.where(visible[None], score, masked)
            top = lax.optimization_barrier(jnp.max(score, axis=-1, keepdims=True))
            weights = jnp.where(visible[None], jnp.exp(score - top), 0.0)
            denom = lax.optimization_barrier(jnp.sum(weights, axis=-1))
            rounded = weights.astype(jnp.bfloat16).astype(jnp.float32)
            summed = jnp.einsum('gqk,kd->gqd', rounded, v_wide)
            return summed / denom[..., None]
        return lax.map(one_block, jnp.arange(blocks, dtype=jnp.int32))
    result = lax.map(one_head, (query_grid, key_grid, value_grid))
    attn = jnp.transpose(result, (1, 3, 0, 2, 4)).reshape(count, q_heads * head_dim).astype(jnp.bfloat16)
    attn_out = jnp.dot(attn, w_out, preferred_element_type=jnp.float32).astype(jnp.bfloat16)
    return (attn_out, key_cache, value_cache)
```

```python
import math

import jax
import jax.numpy as jnp
from jax import lax
from jax.sharding import Mesh
from jax.sharding import PartitionSpec as P

rope_base = 1000000.0
norm_eps = 1e-06
masked = -1e30
max_len = 6144

SEQ = ("z", "x", "ylo")
TEN = ("yhi", "core")


def prompt_starts(lengths, token_pos):
    ends = jnp.cumsum(lengths)
    starts = ends - lengths
    before = (ends[None, :] <= token_pos[:, None]).astype(jnp.int32)
    segment = jnp.sum(before, axis=1)
    onehot = segment[:, None] == jnp.arange(lengths.shape[0], dtype=jnp.int32)[None, :]
    return jnp.sum(jnp.where(onehot, starts[None, :], 0), axis=1)


def head_norm_rope(values, gain, rel_pos):
    width = values.shape[-1]
    half = width // 2
    mean_sq = jnp.mean(values * values, axis=-1, keepdims=True)
    normed = values * lax.rsqrt(mean_sq + norm_eps) * gain
    freq = rope_base ** (-jnp.arange(half, dtype=jnp.float32) * 2.0 / width)
    angle = rel_pos.astype(jnp.float32)[:, None] * freq[None, :]
    cosine = jnp.cos(angle)[:, None, :]
    sine = jnp.sin(angle)[:, None, :]
    first = normed[..., :half]
    second = normed[..., half:]
    return jnp.concatenate(
        [first * cosine - second * sine, second * cosine + first * sine], axis=-1
    )


def on_device(hidden_in, norm_gain, w_query, w_key, w_value, w_out, q_gain, k_gain, lengths):
    tokens = hidden_in.shape[0]
    width = w_query.shape[0]
    head_dim = q_gain.shape[0]
    q_cols = w_query.shape[1]
    kv_cols = w_key.shape[1]
    kv_local = kv_cols // head_dim
    group = q_cols // kv_cols
    combined = jnp.concatenate([w_query, w_key, w_value], axis=1)
    piece = lax.all_gather(hidden_in, TEN, axis=1, tiled=True)
    wide = piece.astype(jnp.float32)
    scaled = (wide * norm_gain[None, :]).astype(jnp.bfloat16)
    acc = jnp.dot(scaled, combined, preferred_element_type=jnp.float32)
    sumsq = jnp.sum(wide * wide, axis=1)
    proj = acc * lax.rsqrt(sumsq / width + norm_eps)[:, None]
    block_index = lax.axis_index(SEQ)
    token_pos = block_index * tokens + jnp.arange(tokens, dtype=jnp.int32)
    seg_start = prompt_starts(lengths, token_pos)
    rel_pos = token_pos - seg_start
    queries = head_norm_rope(
        proj[:, :q_cols].reshape(tokens, kv_local * group, head_dim), q_gain, rel_pos
    ).astype(jnp.bfloat16)
    keys = head_norm_rope(
        proj[:, q_cols : q_cols + kv_cols].reshape(tokens, kv_local, head_dim), k_gain, rel_pos
    ).astype(jnp.bfloat16)
    key_flat = keys.reshape(tokens, kv_cols)
    value_flat = proj[:, q_cols + kv_cols :].astype(jnp.bfloat16)

    kv = jnp.concatenate([key_flat, value_flat], axis=1)
    kv = lax.all_gather(kv, "ylo", axis=0, tiled=True)
    kv = lax.all_gather(kv, "x", axis=0, tiled=True)
    kv = lax.all_gather(kv, "z", axis=0, tiled=True)
    rows = kv.shape[0]
    blocks = rows // tokens
    window = min(blocks, -(-(max_len - 1) // tokens) + 1)
    first_block = jnp.minimum(jnp.min(seg_start) // tokens, blocks - window)
    span = window * tokens
    kv_win = lax.dynamic_slice_in_dim(kv, first_block * tokens, span, 0)
    key_pos = first_block * tokens + jnp.arange(span, dtype=jnp.int32)
    key_heads = kv_win[:, :kv_cols].reshape(span, kv_local, head_dim)
    value_heads = kv_win[:, kv_cols:].reshape(span, kv_local, head_dim)
    query_grid = queries.reshape(tokens, kv_local, group, head_dim)
    inv_root = 1.0 / math.sqrt(head_dim)
    score = (
        jnp.einsum("qhgd,khd->hgqk", query_grid, key_heads, preferred_element_type=jnp.float32)
        * inv_root
    )
    visible = (key_pos[None, :] >= seg_start[:, None]) & (key_pos[None, :] <= token_pos[:, None])
    score = jnp.where(visible[None, None], score, masked)
    top = jnp.max(score, axis=-1, keepdims=True)
    weights = jnp.where(visible[None, None], jnp.exp(score - top), 0.0)
    denom = jnp.sum(weights, axis=-1)
    summed = jnp.einsum(
        "hgqk,khd->hgqd",
        weights.astype(jnp.bfloat16),
        value_heads,
        preferred_element_type=jnp.float32,
    )
    attn = summed / denom[..., None]
    attn = jnp.transpose(attn, (2, 0, 1, 3)).reshape(tokens, q_cols).astype(jnp.bfloat16)
    part = jnp.dot(attn, w_out, preferred_element_type=jnp.float32).astype(jnp.bfloat16)
    nyhi = lax.axis_size("yhi")
    ncore = lax.axis_size("core")
    chunk = tokens // (nyhi * ncore)
    part = part.reshape(nyhi, ncore, chunk, -1).transpose(1, 0, 2, 3).reshape(tokens, -1)
    part = lax.psum_scatter(part, "core", scatter_dimension=0, tiled=True)
    mixed = lax.psum_scatter(part, "yhi", scatter_dimension=0, tiled=True)
    return (mixed, key_flat, value_flat)


def solution(mesh):
    devices = mesh.devices
    nseq, nten = devices.shape
    nz = len({d.coords[2] for d in devices[:, 0]})
    nx = len({d.coords[0] for d in devices[:, 0]})
    ncore = len({d.core_on_chip for d in devices[0, :]})
    split = Mesh(devices.reshape(nz, nx, nseq // (nz * nx), nten // ncore, ncore), SEQ + TEN)
    seq, ten = SEQ, TEN
    placed = (
        P(seq, ten),
        P(),
        P(None, ten),
        P(None, ten),
        P(None, ten),
        P(ten, None),
        P(),
        P(),
        P(),
    )
    return jax.shard_map(
        on_device,
        mesh=split,
        in_specs=placed,
        out_specs=(P(seq + ten, None), P(seq, ten), P(seq, ten)),
        check_vma=False,
    )
```

```python
import math

import jax
import jax.numpy as jnp
from jax import lax
from jax.sharding import Mesh
from jax.sharding import PartitionSpec as P

rope_base = 1000000.0
norm_eps = 1e-06
masked = -1e30
max_len = 6144

SEQ = ("z", "x", "ylo")
TEN = ("yhi", "core")


def prompt_starts(lengths, token_pos):
    ends = jnp.cumsum(lengths)
    starts = ends - lengths
    before = (ends[None, :] <= token_pos[:, None]).astype(jnp.int32)
    segment = jnp.sum(before, axis=1)
    onehot = segment[:, None] == jnp.arange(lengths.shape[0], dtype=jnp.int32)[None, :]
    return jnp.sum(jnp.where(onehot, starts[None, :], 0), axis=1)


def head_norm_rope(values, gain, rel_pos):
    width = values.shape[-1]
    half = width // 2
    mean_sq = jnp.mean(values * values, axis=-1, keepdims=True)
    normed = values * lax.rsqrt(mean_sq + norm_eps) * gain
    freq = rope_base ** (-jnp.arange(half, dtype=jnp.float32) * 2.0 / width)
    angle = rel_pos.astype(jnp.float32)[:, None] * freq[None, :]
    cosine = jnp.cos(angle)[:, None, :]
    sine = jnp.sin(angle)[:, None, :]
    first = normed[..., :half]
    second = normed[..., half:]
    return jnp.concatenate(
        [first * cosine - second * sine, second * cosine + first * sine], axis=-1
    )


def on_device(hidden_in, norm_gain, w_query, w_key, w_value, w_out, q_gain, k_gain, lengths):
    tokens = hidden_in.shape[0]
    width = w_query.shape[0]
    head_dim = q_gain.shape[0]
    q_cols = w_query.shape[1]
    kv_cols = w_key.shape[1]
    kv_local = kv_cols // head_dim
    group = q_cols // kv_cols
    combined = jnp.concatenate([w_query, w_key, w_value], axis=1)
    piece = lax.all_gather(hidden_in, TEN, axis=1, tiled=True)
    wide = piece.astype(jnp.float32)
    scaled = (wide * norm_gain[None, :]).astype(jnp.bfloat16)
    acc = jnp.dot(scaled, combined, preferred_element_type=jnp.float32)
    sumsq = jnp.sum(wide * wide, axis=1)
    proj = acc * lax.rsqrt(sumsq / width + norm_eps)[:, None]
    block_index = lax.axis_index(SEQ)
    token_pos = block_index * tokens + jnp.arange(tokens, dtype=jnp.int32)
    seg_start = prompt_starts(lengths, token_pos)
    rel_pos = token_pos - seg_start
    queries = head_norm_rope(
        proj[:, :q_cols].reshape(tokens, kv_local * group, head_dim), q_gain, rel_pos
    ).astype(jnp.bfloat16)
    keys = head_norm_rope(
        proj[:, q_cols : q_cols + kv_cols].reshape(tokens, kv_local, head_dim), k_gain, rel_pos
    ).astype(jnp.bfloat16)
    key_flat = keys.reshape(tokens, kv_cols)
    value_flat = proj[:, q_cols + kv_cols :].astype(jnp.bfloat16)

    kv = jnp.concatenate([key_flat, value_flat], axis=1)
    kv = lax.all_gather(kv, "ylo", axis=0, tiled=True)
    kv = lax.all_gather(kv, "x", axis=0, tiled=True)
    kv = lax.all_gather(kv, "z", axis=0, tiled=True)
    rows = kv.shape[0]
    blocks = rows // tokens
    window = min(blocks, -(-(max_len - 1) // tokens) + 1)
    first_block = jnp.minimum(jnp.min(seg_start) // tokens, blocks - window)
    span = window * tokens
    kv_win = lax.dynamic_slice_in_dim(kv, first_block * tokens, span, 0)
    key_pos = first_block * tokens + jnp.arange(span, dtype=jnp.int32)
    key_heads = kv_win[:, :kv_cols].reshape(span, kv_local, head_dim)
    value_heads = kv_win[:, kv_cols:].reshape(span, kv_local, head_dim)
    query_grid = queries.reshape(tokens, kv_local, group, head_dim)
    inv_root = 1.0 / math.sqrt(head_dim)
    score = (
        jnp.einsum("qhgd,khd->hgqk", query_grid, key_heads, preferred_element_type=jnp.float32)
        * inv_root
    )
    visible = (key_pos[None, :] >= seg_start[:, None]) & (key_pos[None, :] <= token_pos[:, None])
    score = jnp.where(visible[None, None], score, masked)
    top = jnp.max(score, axis=-1, keepdims=True)
    weights = jnp.where(visible[None, None], jnp.exp(score - top), 0.0)
    denom = jnp.sum(weights, axis=-1)
    summed = jnp.einsum(
        "hgqk,khd->hgqd",
        weights.astype(jnp.bfloat16),
        value_heads,
        preferred_element_type=jnp.float32,
    )
    attn = summed / denom[..., None]
    attn = jnp.transpose(attn, (2, 0, 1, 3)).reshape(tokens, q_cols).astype(jnp.bfloat16)
    part = jnp.dot(attn, w_out, preferred_element_type=jnp.float32).astype(jnp.bfloat16)
    nyhi = lax.axis_size("yhi")
    ncore = lax.axis_size("core")
    chunk = tokens // (nyhi * ncore)
    part = part.reshape(nyhi, ncore, chunk, -1).transpose(1, 0, 2, 3)
    part = lax.all_to_all(part, "core", 0, 0, tiled=True)
    part = jnp.sum(part.astype(jnp.float32), axis=0).astype(jnp.bfloat16)
    part = lax.all_to_all(part, "yhi", 0, 0, tiled=True)
    mixed = jnp.sum(part.astype(jnp.float32), axis=0).astype(jnp.bfloat16)
    return (mixed, key_flat, value_flat)


def solution(mesh):
    devices = mesh.devices
    nseq, nten = devices.shape
    nz = len({d.coords[2] for d in devices[:, 0]})
    nx = len({d.coords[0] for d in devices[:, 0]})
    ncore = len({d.core_on_chip for d in devices[0, :]})
    split = Mesh(devices.reshape(nz, nx, nseq // (nz * nx), nten // ncore, ncore), SEQ + TEN)
    seq, ten = SEQ, TEN
    placed = (
        P(seq, ten),
        P(),
        P(None, ten),
        P(None, ten),
        P(None, ten),
        P(ten, None),
        P(),
        P(),
        P(),
    )
    return jax.shard_map(
        on_device,
        mesh=split,
        in_specs=placed,
        out_specs=(P(seq + ten, None), P(seq, ten), P(seq, ten)),
        check_vma=False,
    )
```

```python
import math

import jax
import jax.numpy as jnp
from jax import lax
from jax.sharding import Mesh
from jax.sharding import PartitionSpec as P

rope_base = 1000000.0
norm_eps = 1e-06
masked = -1e30
max_len = 6144

SEQ = ("z", "x", "ylo")
TEN = ("yhi", "core")


def prompt_starts(lengths, token_pos):
    ends = jnp.cumsum(lengths)
    starts = ends - lengths
    before = (ends[None, :] <= token_pos[:, None]).astype(jnp.int32)
    segment = jnp.sum(before, axis=1)
    onehot = segment[:, None] == jnp.arange(lengths.shape[0], dtype=jnp.int32)[None, :]
    return jnp.sum(jnp.where(onehot, starts[None, :], 0), axis=1)


def head_norm_rope(values, gain, rel_pos):
    width = values.shape[-1]
    half = width // 2
    mean_sq = jnp.mean(values * values, axis=-1, keepdims=True)
    normed = values * lax.rsqrt(mean_sq + norm_eps) * gain
    freq = rope_base ** (-jnp.arange(half, dtype=jnp.float32) * 2.0 / width)
    angle = rel_pos.astype(jnp.float32)[:, None] * freq[None, :]
    cosine = jnp.cos(angle)[:, None, :]
    sine = jnp.sin(angle)[:, None, :]
    first = normed[..., :half]
    second = normed[..., half:]
    return jnp.concatenate(
        [first * cosine - second * sine, second * cosine + first * sine], axis=-1
    )


def on_device(hidden_in, norm_gain, w_query, w_key, w_value, w_out, q_gain, k_gain, lengths):
    tokens = hidden_in.shape[0]
    width = w_query.shape[0]
    head_dim = q_gain.shape[0]
    q_cols = w_query.shape[1]
    kv_cols = w_key.shape[1]
    kv_local = kv_cols // head_dim
    group = q_cols // kv_cols
    combined = jnp.concatenate([w_query, w_key, w_value], axis=1)
    piece = lax.all_gather(hidden_in, TEN, axis=1, tiled=True)
    wide = piece.astype(jnp.float32)
    scaled = (wide * norm_gain[None, :]).astype(jnp.bfloat16)
    acc = jnp.dot(scaled, combined, preferred_element_type=jnp.float32)
    sumsq = jnp.sum(wide * wide, axis=1)
    proj = acc * lax.rsqrt(sumsq / width + norm_eps)[:, None]
    block_index = lax.axis_index(SEQ)
    token_pos = block_index * tokens + jnp.arange(tokens, dtype=jnp.int32)
    seg_start = prompt_starts(lengths, token_pos)
    rel_pos = token_pos - seg_start
    queries = head_norm_rope(
        proj[:, :q_cols].reshape(tokens, kv_local * group, head_dim), q_gain, rel_pos
    ).astype(jnp.bfloat16)
    keys = head_norm_rope(
        proj[:, q_cols : q_cols + kv_cols].reshape(tokens, kv_local, head_dim), k_gain, rel_pos
    ).astype(jnp.bfloat16)
    key_flat = keys.reshape(tokens, kv_cols)
    value_flat = proj[:, q_cols + kv_cols :].astype(jnp.bfloat16)

    nz, nx, nlo = lax.axis_size("z"), lax.axis_size("x"), lax.axis_size("ylo")
    kg = lax.all_gather(key_flat, "ylo", axis=0, tiled=True)
    kg = lax.all_gather(kg, "x", axis=0, tiled=True)
    kg = lax.all_gather(kg, "z", axis=0, tiled=True)
    vg = lax.all_gather(value_flat, "z", axis=0, tiled=False)
    vg = lax.all_gather(vg, "ylo", axis=1, tiled=False)
    vg = jnp.broadcast_to(vg[None], (nx,) + vg.shape)
    vg = lax.all_to_all(vg, "x", 0, 1, tiled=False)
    vg = vg.reshape(nz * nx * nlo * tokens, kv_cols)
    kv = jnp.concatenate([kg, vg], axis=1)
    rows = kv.shape[0]
    blocks = rows // tokens
    window = min(blocks, -(-(max_len - 1) // tokens) + 1)
    first_block = jnp.minimum(jnp.min(seg_start) // tokens, blocks - window)
    span = window * tokens
    kv_win = lax.dynamic_slice_in_dim(kv, first_block * tokens, span, 0)
    key_pos = first_block * tokens + jnp.arange(span, dtype=jnp.int32)
    key_heads = kv_win[:, :kv_cols].reshape(span, kv_local, head_dim)
    value_heads = kv_win[:, kv_cols:].reshape(span, kv_local, head_dim)
    query_grid = queries.reshape(tokens, kv_local, group, head_dim)
    inv_root = 1.0 / math.sqrt(head_dim)
    score = (
        jnp.einsum("qhgd,khd->hgqk", query_grid, key_heads, preferred_element_type=jnp.float32)
        * inv_root
    )
    visible = (key_pos[None, :] >= seg_start[:, None]) & (key_pos[None, :] <= token_pos[:, None])
    score = jnp.where(visible[None, None], score, masked)
    top = jnp.max(score, axis=-1, keepdims=True)
    weights = jnp.where(visible[None, None], jnp.exp(score - top), 0.0)
    denom = jnp.sum(weights, axis=-1)
    summed = jnp.einsum(
        "hgqk,khd->hgqd",
        weights.astype(jnp.bfloat16),
        value_heads,
        preferred_element_type=jnp.float32,
    )
    attn = summed / denom[..., None]
    attn = jnp.transpose(attn, (2, 0, 1, 3)).reshape(tokens, q_cols).astype(jnp.bfloat16)
    part = jnp.dot(attn, w_out, preferred_element_type=jnp.float32).astype(jnp.bfloat16)
    nyhi = lax.axis_size("yhi")
    ncore = lax.axis_size("core")
    chunk = tokens // (nyhi * ncore)
    part = part.reshape(nyhi, ncore, chunk, -1).transpose(1, 0, 2, 3)
    part = lax.all_to_all(part, "core", 0, 0, tiled=True)
    part = jnp.sum(part.astype(jnp.float32), axis=0).astype(jnp.bfloat16)
    part = lax.all_to_all(part, "yhi", 0, 0, tiled=True)
    mixed = jnp.sum(part.astype(jnp.float32), axis=0).astype(jnp.bfloat16)
    return (mixed, key_flat, value_flat)


def solution(mesh):
    devices = mesh.devices
    nseq, nten = devices.shape
    nz = len({d.coords[2] for d in devices[:, 0]})
    nx = len({d.coords[0] for d in devices[:, 0]})
    ncore = len({d.core_on_chip for d in devices[0, :]})
    split = Mesh(devices.reshape(nz, nx, nseq // (nz * nx), nten // ncore, ncore), SEQ + TEN)
    seq, ten = SEQ, TEN
    placed = (
        P(seq, ten),
        P(),
        P(None, ten),
        P(None, ten),
        P(None, ten),
        P(ten, None),
        P(),
        P(),
        P(),
    )
    return jax.shard_map(
        on_device,
        mesh=split,
        in_specs=placed,
        out_specs=(P(seq + ten, None), P(seq, ten), P(seq, ten)),
        check_vma=False,
    )
```

```python
import math

import jax
import jax.numpy as jnp
from jax import lax
from jax.sharding import Mesh
from jax.sharding import PartitionSpec as P

rope_base = 1000000.0
norm_eps = 1e-06
masked = -1e30
max_len = 6144

SEQ = ("z", "x", "ylo")
TEN = ("yhi", "core")


def prompt_starts(lengths, token_pos):
    ends = jnp.cumsum(lengths)
    starts = ends - lengths
    before = (ends[None, :] <= token_pos[:, None]).astype(jnp.int32)
    segment = jnp.sum(before, axis=1)
    onehot = segment[:, None] == jnp.arange(lengths.shape[0], dtype=jnp.int32)[None, :]
    return jnp.sum(jnp.where(onehot, starts[None, :], 0), axis=1)


def head_norm_rope(values, gain, rel_pos):
    width = values.shape[-1]
    half = width // 2
    mean_sq = jnp.mean(values * values, axis=-1, keepdims=True)
    normed = values * lax.rsqrt(mean_sq + norm_eps) * gain
    freq = rope_base ** (-jnp.arange(half, dtype=jnp.float32) * 2.0 / width)
    angle = rel_pos.astype(jnp.float32)[:, None] * freq[None, :]
    cosine = jnp.cos(angle)[:, None, :]
    sine = jnp.sin(angle)[:, None, :]
    first = normed[..., :half]
    second = normed[..., half:]
    return jnp.concatenate(
        [first * cosine - second * sine, second * cosine + first * sine], axis=-1
    )


def ring_gather(piece, inner, name, stride):
    n = lax.axis_size(name)
    c = lax.axis_index(name)
    cw = [(i, (i + 1) % n) for i in range(n)]
    ccw = [(i, (i - 1) % n) for i in range(n)]
    pieces, ids = [piece], [c * stride + inner]
    a = b = piece
    for s in range(1, (n - 1) // 2 + 1):
        a = lax.ppermute(a, name, cw)
        b = lax.ppermute(b, name, ccw)
        pieces += [a, b]
        ids += [((c - s) % n) * stride + inner, ((c + s) % n) * stride + inner]
    if n % 2 == 0:
        far = ((c + n // 2) % n) * stride
        m = piece.shape[0]
        if m % 2 == 0:
            pieces += [lax.ppermute(a[: m // 2], name, cw), lax.ppermute(b[m // 2 :], name, ccw)]
            ids += [far + inner[: m // 2], far + inner[m // 2 :]]
        else:
            pieces += [lax.ppermute(a, name, cw)]
            ids += [far + inner]
    return jnp.concatenate(pieces, axis=0), jnp.concatenate(ids, axis=0)


def on_device(hidden_in, norm_gain, w_query, w_key, w_value, w_out, q_gain, k_gain, lengths):
    tokens = hidden_in.shape[0]
    width = w_query.shape[0]
    head_dim = q_gain.shape[0]
    q_cols = w_query.shape[1]
    kv_cols = w_key.shape[1]
    kv_local = kv_cols // head_dim
    group = q_cols // kv_cols
    combined = jnp.concatenate([w_query, w_key, w_value], axis=1)
    piece = lax.all_gather(hidden_in, TEN, axis=1, tiled=True)
    wide = piece.astype(jnp.float32)
    scaled = (wide * norm_gain[None, :]).astype(jnp.bfloat16)
    acc = jnp.dot(scaled, combined, preferred_element_type=jnp.float32)
    sumsq = jnp.sum(wide * wide, axis=1)
    proj = acc * lax.rsqrt(sumsq / width + norm_eps)[:, None]
    block_index = lax.axis_index(SEQ)
    token_pos = block_index * tokens + jnp.arange(tokens, dtype=jnp.int32)
    seg_start = prompt_starts(lengths, token_pos)
    rel_pos = token_pos - seg_start
    queries = head_norm_rope(
        proj[:, :q_cols].reshape(tokens, kv_local * group, head_dim), q_gain, rel_pos
    ).astype(jnp.bfloat16)
    keys = head_norm_rope(
        proj[:, q_cols : q_cols + kv_cols].reshape(tokens, kv_local, head_dim), k_gain, rel_pos
    ).astype(jnp.bfloat16)
    key_flat = keys.reshape(tokens, kv_cols)
    value_flat = proj[:, q_cols + kv_cols :].astype(jnp.bfloat16)

    nx, nlo = lax.axis_size("x"), lax.axis_size("ylo")
    piece = jnp.concatenate([key_flat, value_flat], axis=1)[None]
    block_ids = jnp.zeros((1,), jnp.int32)
    piece, block_ids = ring_gather(piece, block_ids, "ylo", 1)
    piece, block_ids = ring_gather(piece, block_ids, "x", nlo)
    piece, block_ids = ring_gather(piece, block_ids, "z", nx * nlo)
    span = piece.shape[0] * tokens
    kv_all = piece.reshape(span, 2 * kv_cols)
    key_pos = (block_ids[:, None] * tokens + jnp.arange(tokens, dtype=jnp.int32)[None, :]).reshape(span)
    key_heads = kv_all[:, :kv_cols].reshape(span, kv_local, head_dim)
    value_heads = kv_all[:, kv_cols:].reshape(span, kv_local, head_dim)
    query_grid = queries.reshape(tokens, kv_local, group, head_dim)
    inv_root = 1.0 / math.sqrt(head_dim)
    score = (
        jnp.einsum("qhgd,khd->hgqk", query_grid, key_heads, preferred_element_type=jnp.float32)
        * inv_root
    )
    visible = (key_pos[None, :] >= seg_start[:, None]) & (key_pos[None, :] <= token_pos[:, None])
    score = jnp.where(visible[None, None], score, masked)
    top = jnp.max(score, axis=-1, keepdims=True)
    weights = jnp.where(visible[None, None], jnp.exp(score - top), 0.0)
    denom = jnp.sum(weights, axis=-1)
    summed = jnp.einsum(
        "hgqk,khd->hgqd",
        weights.astype(jnp.bfloat16),
        value_heads,
        preferred_element_type=jnp.float32,
    )
    attn = summed / denom[..., None]
    attn = jnp.transpose(attn, (2, 0, 1, 3)).reshape(tokens, q_cols).astype(jnp.bfloat16)
    part = jnp.dot(attn, w_out, preferred_element_type=jnp.float32).astype(jnp.bfloat16)
    nyhi = lax.axis_size("yhi")
    ncore = lax.axis_size("core")
    chunk = tokens // (nyhi * ncore)
    part = part.reshape(nyhi, ncore, chunk, -1).transpose(1, 0, 2, 3)
    part = lax.all_to_all(part, "core", 0, 0, tiled=True)
    part = jnp.sum(part.astype(jnp.float32), axis=0).astype(jnp.bfloat16)
    part = lax.all_to_all(part, "yhi", 0, 0, tiled=True)
    mixed = jnp.sum(part.astype(jnp.float32), axis=0).astype(jnp.bfloat16)
    return (mixed, key_flat, value_flat)


def solution(mesh):
    devices = mesh.devices
    nseq, nten = devices.shape
    nz = len({d.coords[2] for d in devices[:, 0]})
    nx = len({d.coords[0] for d in devices[:, 0]})
    ncore = len({d.core_on_chip for d in devices[0, :]})
    split = Mesh(devices.reshape(nz, nx, nseq // (nz * nx), nten // ncore, ncore), SEQ + TEN)
    seq, ten = SEQ, TEN
    placed = (
        P(seq, ten),
        P(),
        P(None, ten),
        P(None, ten),
        P(None, ten),
        P(ten, None),
        P(),
        P(),
        P(),
    )
    return jax.shard_map(
        on_device,
        mesh=split,
        in_specs=placed,
        out_specs=(P(seq + ten, None), P(seq, ten), P(seq, ten)),
        check_vma=False,
    )
```

```python
import math

import jax
import jax.numpy as jnp
from jax import lax
from jax.sharding import Mesh
from jax.sharding import PartitionSpec as P

rope_base = 1000000.0
norm_eps = 1e-06
masked = -1e30
max_len = 6144

SEQ = ("z", "x", "ylo")
TEN = ("yhi", "core")


def prompt_starts(lengths, token_pos):
    ends = jnp.cumsum(lengths)
    starts = ends - lengths
    before = (ends[None, :] <= token_pos[:, None]).astype(jnp.int32)
    segment = jnp.sum(before, axis=1)
    onehot = segment[:, None] == jnp.arange(lengths.shape[0], dtype=jnp.int32)[None, :]
    return jnp.sum(jnp.where(onehot, starts[None, :], 0), axis=1)


def head_norm_rope(values, gain, rel_pos):
    width = values.shape[-1]
    half = width // 2
    mean_sq = jnp.mean(values * values, axis=-1, keepdims=True)
    normed = values * lax.rsqrt(mean_sq + norm_eps) * gain
    freq = rope_base ** (-jnp.arange(half, dtype=jnp.float32) * 2.0 / width)
    angle = rel_pos.astype(jnp.float32)[:, None] * freq[None, :]
    cosine = jnp.cos(angle)[:, None, :]
    sine = jnp.sin(angle)[:, None, :]
    first = normed[..., :half]
    second = normed[..., half:]
    return jnp.concatenate(
        [first * cosine - second * sine, second * cosine + first * sine], axis=-1
    )


def ring_gather(piece, inner, name, stride):
    n = lax.axis_size(name)
    c = lax.axis_index(name)
    cw = [(i, (i + 1) % n) for i in range(n)]
    ccw = [(i, (i - 1) % n) for i in range(n)]
    pieces, ids = [piece], [c * stride + inner]
    a = b = piece
    for s in range(1, (n - 1) // 2 + 1):
        a = lax.ppermute(a, name, cw)
        b = lax.ppermute(b, name, ccw)
        pieces += [a, b]
        ids += [((c - s) % n) * stride + inner, ((c + s) % n) * stride + inner]
    if n % 2 == 0:
        far = ((c + n // 2) % n) * stride
        m = piece.shape[0]
        if m % 2 == 0:
            pieces += [lax.ppermute(a[: m // 2], name, cw), lax.ppermute(b[m // 2 :], name, ccw)]
            ids += [far + inner[: m // 2], far + inner[m // 2 :]]
        else:
            pieces += [lax.ppermute(a, name, cw)]
            ids += [far + inner]
    return jnp.concatenate(pieces, axis=0), jnp.concatenate(ids, axis=0)


def on_device(hidden_in, norm_gain, w_query, w_key, w_value, w_out, q_gain, k_gain, lengths):
    tokens = hidden_in.shape[0]
    width = w_query.shape[0]
    head_dim = q_gain.shape[0]
    q_cols = w_query.shape[1]
    kv_cols = w_key.shape[1]
    kv_local = kv_cols // head_dim
    group = q_cols // kv_cols
    combined = jnp.concatenate([w_query, w_key, w_value], axis=1)
    piece = lax.all_gather(hidden_in, TEN, axis=1, tiled=True)
    wide = piece.astype(jnp.float32)
    scaled = (wide * norm_gain[None, :]).astype(jnp.bfloat16)
    acc = jnp.dot(scaled, combined, preferred_element_type=jnp.float32)
    sumsq = jnp.sum(wide * wide, axis=1)
    proj = acc * lax.rsqrt(sumsq / width + norm_eps)[:, None]
    block_index = lax.axis_index(SEQ)
    token_pos = block_index * tokens + jnp.arange(tokens, dtype=jnp.int32)
    seg_start = prompt_starts(lengths, token_pos)
    rel_pos = token_pos - seg_start
    queries = head_norm_rope(
        proj[:, :q_cols].reshape(tokens, kv_local * group, head_dim), q_gain, rel_pos
    ).astype(jnp.bfloat16)
    keys = head_norm_rope(
        proj[:, q_cols : q_cols + kv_cols].reshape(tokens, kv_local, head_dim), k_gain, rel_pos
    ).astype(jnp.bfloat16)
    key_flat = keys.reshape(tokens, kv_cols)
    value_flat = proj[:, q_cols + kv_cols :].astype(jnp.bfloat16)

    nx, nlo = lax.axis_size("x"), lax.axis_size("ylo")
    piece = jnp.concatenate([key_flat, value_flat], axis=1)[None]
    block_ids = jnp.zeros((1,), jnp.int32)
    plane = nx * nlo
    piece = lax.all_to_all(jnp.broadcast_to(piece, (plane,) + piece.shape[1:]), ("x", "ylo"), 0, 0, tiled=True)
    block_ids = jnp.arange(plane, dtype=jnp.int32)
    piece, block_ids = ring_gather(piece, block_ids, "z", nx * nlo)
    span = piece.shape[0] * tokens
    kv_all = piece.reshape(span, 2 * kv_cols)
    key_pos = (block_ids[:, None] * tokens + jnp.arange(tokens, dtype=jnp.int32)[None, :]).reshape(span)
    key_heads = kv_all[:, :kv_cols].reshape(span, kv_local, head_dim)
    value_heads = kv_all[:, kv_cols:].reshape(span, kv_local, head_dim)
    query_grid = queries.reshape(tokens, kv_local, group, head_dim)
    inv_root = 1.0 / math.sqrt(head_dim)
    score = (
        jnp.einsum("qhgd,khd->hgqk", query_grid, key_heads, preferred_element_type=jnp.float32)
        * inv_root
    )
    visible = (key_pos[None, :] >= seg_start[:, None]) & (key_pos[None, :] <= token_pos[:, None])
    score = jnp.where(visible[None, None], score, masked)
    top = jnp.max(score, axis=-1, keepdims=True)
    weights = jnp.where(visible[None, None], jnp.exp(score - top), 0.0)
    denom = jnp.sum(weights, axis=-1)
    summed = jnp.einsum(
        "hgqk,khd->hgqd",
        weights.astype(jnp.bfloat16),
        value_heads,
        preferred_element_type=jnp.float32,
    )
    attn = summed / denom[..., None]
    attn = jnp.transpose(attn, (2, 0, 1, 3)).reshape(tokens, q_cols).astype(jnp.bfloat16)
    part = jnp.dot(attn, w_out, preferred_element_type=jnp.float32).astype(jnp.bfloat16)
    nyhi = lax.axis_size("yhi")
    ncore = lax.axis_size("core")
    chunk = tokens // (nyhi * ncore)
    part = part.reshape(nyhi, ncore, chunk, -1).transpose(1, 0, 2, 3)
    part = lax.all_to_all(part, "core", 0, 0, tiled=True)
    part = jnp.sum(part.astype(jnp.float32), axis=0).astype(jnp.bfloat16)
    part = lax.all_to_all(part, "yhi", 0, 0, tiled=True)
    mixed = jnp.sum(part.astype(jnp.float32), axis=0).astype(jnp.bfloat16)
    return (mixed, key_flat, value_flat)


def solution(mesh):
    devices = mesh.devices
    nseq, nten = devices.shape
    nz = len({d.coords[2] for d in devices[:, 0]})
    nx = len({d.coords[0] for d in devices[:, 0]})
    ncore = len({d.core_on_chip for d in devices[0, :]})
    split = Mesh(devices.reshape(nz, nx, nseq // (nz * nx), nten // ncore, ncore), SEQ + TEN)
    seq, ten = SEQ, TEN
    placed = (
        P(seq, ten),
        P(),
        P(None, ten),
        P(None, ten),
        P(None, ten),
        P(ten, None),
        P(),
        P(),
        P(),
    )
    return jax.shard_map(
        on_device,
        mesh=split,
        in_specs=placed,
        out_specs=(P(seq + ten, None), P(seq, ten), P(seq, ten)),
        check_vma=False,
    )
```

```python
import math

import jax
import jax.numpy as jnp
from jax import lax
from jax.sharding import Mesh
from jax.sharding import PartitionSpec as P

rope_base = 1000000.0
norm_eps = 1e-06
masked = -1e30
max_len = 6144

SEQ = ("z", "x", "ylo")
TEN = ("yhi", "core")


def prompt_starts(lengths, token_pos):
    ends = jnp.cumsum(lengths)
    starts = ends - lengths
    before = (ends[None, :] <= token_pos[:, None]).astype(jnp.int32)
    segment = jnp.sum(before, axis=1)
    onehot = segment[:, None] == jnp.arange(lengths.shape[0], dtype=jnp.int32)[None, :]
    return jnp.sum(jnp.where(onehot, starts[None, :], 0), axis=1)


def head_norm_rope(values, gain, rel_pos):
    width = values.shape[-1]
    half = width // 2
    mean_sq = jnp.mean(values * values, axis=-1, keepdims=True)
    normed = values * lax.rsqrt(mean_sq + norm_eps) * gain
    freq = rope_base ** (-jnp.arange(half, dtype=jnp.float32) * 2.0 / width)
    angle = rel_pos.astype(jnp.float32)[:, None] * freq[None, :]
    cosine = jnp.cos(angle)[:, None, :]
    sine = jnp.sin(angle)[:, None, :]
    first = normed[..., :half]
    second = normed[..., half:]
    return jnp.concatenate(
        [first * cosine - second * sine, second * cosine + first * sine], axis=-1
    )


def ring_gather(piece, inner, name, stride):
    n = lax.axis_size(name)
    c = lax.axis_index(name)
    cw = [(i, (i + 1) % n) for i in range(n)]
    ccw = [(i, (i - 1) % n) for i in range(n)]
    pieces, ids = [piece], [c * stride + inner]
    a = b = piece
    for s in range(1, (n - 1) // 2 + 1):
        a = lax.ppermute(a, name, cw)
        b = lax.ppermute(b, name, ccw)
        pieces += [a, b]
        ids += [((c - s) % n) * stride + inner, ((c + s) % n) * stride + inner]
    if n % 2 == 0:
        far = ((c + n // 2) % n) * stride
        m = piece.shape[0]
        if m % 2 == 0:
            pieces += [lax.ppermute(a[: m // 2], name, cw), lax.ppermute(b[m // 2 :], name, ccw)]
            ids += [far + inner[: m // 2], far + inner[m // 2 :]]
        else:
            pieces += [lax.ppermute(a, name, cw)]
            ids += [far + inner]
    return jnp.concatenate(pieces, axis=0), jnp.concatenate(ids, axis=0)


def on_device(hidden_in, norm_gain, w_query, w_key, w_value, w_out, q_gain, k_gain, lengths):
    tokens = hidden_in.shape[0]
    width = w_query.shape[0]
    head_dim = q_gain.shape[0]
    q_cols = w_query.shape[1]
    kv_cols = w_key.shape[1]
    kv_local = kv_cols // head_dim
    group = q_cols // kv_cols
    combined = jnp.concatenate([w_query, w_key, w_value], axis=1)
    piece = lax.all_gather(hidden_in, TEN, axis=1, tiled=True)
    wide = piece.astype(jnp.float32)
    scaled = (wide * norm_gain[None, :]).astype(jnp.bfloat16)
    acc = jnp.dot(scaled, combined, preferred_element_type=jnp.float32)
    sumsq = jnp.sum(wide * wide, axis=1)
    proj = acc * lax.rsqrt(sumsq / width + norm_eps)[:, None]
    block_index = lax.axis_index(SEQ)
    token_pos = block_index * tokens + jnp.arange(tokens, dtype=jnp.int32)
    seg_start = prompt_starts(lengths, token_pos)
    rel_pos = token_pos - seg_start
    queries = head_norm_rope(
        proj[:, :q_cols].reshape(tokens, kv_local * group, head_dim), q_gain, rel_pos
    ).astype(jnp.bfloat16)
    keys = head_norm_rope(
        proj[:, q_cols : q_cols + kv_cols].reshape(tokens, kv_local, head_dim), k_gain, rel_pos
    ).astype(jnp.bfloat16)
    key_flat = keys.reshape(tokens, kv_cols)
    value_flat = proj[:, q_cols + kv_cols :].astype(jnp.bfloat16)

    nx, nlo = lax.axis_size("x"), lax.axis_size("ylo")
    plane = nx * nlo
    kp = lax.all_to_all(jnp.broadcast_to(key_flat[None], (plane, tokens, kv_cols)), ("x", "ylo"), 0, 0, tiled=True)
    kp, block_ids = ring_gather(kp, jnp.arange(plane, dtype=jnp.int32), "z", plane)
    vz, unused = ring_gather(value_flat[None], jnp.zeros((1,), jnp.int32), "z", plane)
    vp = lax.all_to_all(jnp.broadcast_to(vz[None], (plane,) + vz.shape), ("x", "ylo"), 0, 0, tiled=False)
    vp = jnp.swapaxes(vp, 0, 1)
    span = kp.shape[0] * tokens
    key_pos = (block_ids[:, None] * tokens + jnp.arange(tokens, dtype=jnp.int32)[None, :]).reshape(span)
    key_heads = kp.reshape(span, kv_local, head_dim)
    value_heads = vp.reshape(span, kv_local, head_dim)
    query_grid = queries.reshape(tokens, kv_local, group, head_dim)
    inv_root = 1.0 / math.sqrt(head_dim)
    score = (
        jnp.einsum("qhgd,khd->hgqk", query_grid, key_heads, preferred_element_type=jnp.float32)
        * inv_root
    )
    visible = (key_pos[None, :] >= seg_start[:, None]) & (key_pos[None, :] <= token_pos[:, None])
    score = jnp.where(visible[None, None], score, masked)
    top = jnp.max(score, axis=-1, keepdims=True)
    weights = jnp.where(visible[None, None], jnp.exp(score - top), 0.0)
    denom = jnp.sum(weights, axis=-1)
    summed = jnp.einsum(
        "hgqk,khd->hgqd",
        weights.astype(jnp.bfloat16),
        value_heads,
        preferred_element_type=jnp.float32,
    )
    attn = summed / denom[..., None]
    attn = jnp.transpose(attn, (2, 0, 1, 3)).reshape(tokens, q_cols).astype(jnp.bfloat16)
    part = jnp.dot(attn, w_out, preferred_element_type=jnp.float32).astype(jnp.bfloat16)
    nyhi = lax.axis_size("yhi")
    ncore = lax.axis_size("core")
    chunk = tokens // (nyhi * ncore)
    part = part.reshape(nyhi, ncore, chunk, -1).transpose(1, 0, 2, 3)
    part = lax.all_to_all(part, "core", 0, 0, tiled=True)
    part = jnp.sum(part.astype(jnp.float32), axis=0).astype(jnp.bfloat16)
    part = lax.all_to_all(part, "yhi", 0, 0, tiled=True)
    mixed = jnp.sum(part.astype(jnp.float32), axis=0).astype(jnp.bfloat16)
    return (mixed, key_flat, value_flat)


def solution(mesh):
    devices = mesh.devices
    nseq, nten = devices.shape
    nz = len({d.coords[2] for d in devices[:, 0]})
    nx = len({d.coords[0] for d in devices[:, 0]})
    ncore = len({d.core_on_chip for d in devices[0, :]})
    split = Mesh(devices.reshape(nz, nx, nseq // (nz * nx), nten // ncore, ncore), SEQ + TEN)
    seq, ten = SEQ, TEN
    placed = (
        P(seq, ten),
        P(),
        P(None, ten),
        P(None, ten),
        P(None, ten),
        P(ten, None),
        P(),
        P(),
        P(),
    )
    return jax.shard_map(
        on_device,
        mesh=split,
        in_specs=placed,
        out_specs=(P(seq + ten, None), P(seq, ten), P(seq, ten)),
        check_vma=False,
    )
```

```python
import math

import jax
import jax.numpy as jnp
from jax import lax
from jax.sharding import Mesh
from jax.sharding import PartitionSpec as P

rope_base = 1000000.0
norm_eps = 1e-06
masked = -1e30
max_len = 6144

SEQ = ("z", "x", "ylo")
TEN = ("yhi", "core")


def prompt_starts(lengths, token_pos):
    ends = jnp.cumsum(lengths)
    starts = ends - lengths
    before = (ends[None, :] <= token_pos[:, None]).astype(jnp.int32)
    segment = jnp.sum(before, axis=1)
    onehot = segment[:, None] == jnp.arange(lengths.shape[0], dtype=jnp.int32)[None, :]
    return jnp.sum(jnp.where(onehot, starts[None, :], 0), axis=1)


def head_norm_rope(values, gain, rel_pos):
    width = values.shape[-1]
    half = width // 2
    mean_sq = jnp.mean(values * values, axis=-1, keepdims=True)
    normed = values * lax.rsqrt(mean_sq + norm_eps) * gain
    freq = rope_base ** (-jnp.arange(half, dtype=jnp.float32) * 2.0 / width)
    angle = rel_pos.astype(jnp.float32)[:, None] * freq[None, :]
    cosine = jnp.cos(angle)[:, None, :]
    sine = jnp.sin(angle)[:, None, :]
    first = normed[..., :half]
    second = normed[..., half:]
    return jnp.concatenate(
        [first * cosine - second * sine, second * cosine + first * sine], axis=-1
    )


def ring_gather(piece, inner, name, stride):
    n = lax.axis_size(name)
    c = lax.axis_index(name)
    cw = [(i, (i + 1) % n) for i in range(n)]
    ccw = [(i, (i - 1) % n) for i in range(n)]
    pieces, ids = [piece], [c * stride + inner]
    a = b = piece
    for s in range(1, (n - 1) // 2 + 1):
        a = lax.ppermute(a, name, cw)
        b = lax.ppermute(b, name, ccw)
        pieces += [a, b]
        ids += [((c - s) % n) * stride + inner, ((c + s) % n) * stride + inner]
    if n % 2 == 0:
        far = ((c + n // 2) % n) * stride
        m = piece.shape[0]
        if m % 2 == 0:
            pieces += [lax.ppermute(a[: m // 2], name, cw), lax.ppermute(b[m // 2 :], name, ccw)]
            ids += [far + inner[: m // 2], far + inner[m // 2 :]]
        else:
            pieces += [lax.ppermute(a, name, cw)]
            ids += [far + inner]
    return jnp.concatenate(pieces, axis=0), jnp.concatenate(ids, axis=0)


def on_device(hidden_in, norm_gain, w_query, w_key, w_value, w_out, q_gain, k_gain, lengths):
    tokens = hidden_in.shape[0]
    width = w_query.shape[0]
    head_dim = q_gain.shape[0]
    q_cols = w_query.shape[1]
    kv_cols = w_key.shape[1]
    kv_local = kv_cols // head_dim
    group = q_cols // kv_cols
    combined = jnp.concatenate([w_query, w_key, w_value], axis=1)
    cols = lax.axis_size(TEN)
    piece = lax.all_to_all(jnp.broadcast_to(hidden_in[None], (cols,) + hidden_in.shape), TEN, 0, 0, tiled=True)
    wide = piece.astype(jnp.float32)
    scaled = (wide * norm_gain.reshape(cols, 1, -1)).astype(jnp.bfloat16)
    acc = jnp.einsum(
        "jtc,jcn->tn", scaled, combined.reshape(cols, -1, combined.shape[1]),
        preferred_element_type=jnp.float32,
    )
    sumsq = jnp.sum(wide * wide, axis=(0, 2))
    proj = acc * lax.rsqrt(sumsq / width + norm_eps)[:, None]
    block_index = lax.axis_index(SEQ)
    token_pos = block_index * tokens + jnp.arange(tokens, dtype=jnp.int32)
    seg_start = prompt_starts(lengths, token_pos)
    rel_pos = token_pos - seg_start
    queries = head_norm_rope(
        proj[:, :q_cols].reshape(tokens, kv_local * group, head_dim), q_gain, rel_pos
    ).astype(jnp.bfloat16)
    keys = head_norm_rope(
        proj[:, q_cols : q_cols + kv_cols].reshape(tokens, kv_local, head_dim), k_gain, rel_pos
    ).astype(jnp.bfloat16)
    key_flat = keys.reshape(tokens, kv_cols)
    value_flat = proj[:, q_cols + kv_cols :].astype(jnp.bfloat16)

    nx, nlo = lax.axis_size("x"), lax.axis_size("ylo")
    piece = jnp.concatenate([key_flat, value_flat], axis=1)[None]
    block_ids = jnp.zeros((1,), jnp.int32)
    plane = nx * nlo
    piece = lax.all_to_all(jnp.broadcast_to(piece, (plane,) + piece.shape[1:]), ("x", "ylo"), 0, 0, tiled=True)
    block_ids = jnp.arange(plane, dtype=jnp.int32)
    piece, block_ids = ring_gather(piece, block_ids, "z", nx * nlo)
    span = piece.shape[0] * tokens
    kv_all = piece.reshape(span, 2 * kv_cols)
    key_pos = (block_ids[:, None] * tokens + jnp.arange(tokens, dtype=jnp.int32)[None, :]).reshape(span)
    key_heads = kv_all[:, :kv_cols].reshape(span, kv_local, head_dim)
    value_heads = kv_all[:, kv_cols:].reshape(span, kv_local, head_dim)
    query_grid = queries.reshape(tokens, kv_local, group, head_dim)
    inv_root = 1.0 / math.sqrt(head_dim)
    score = (
        jnp.einsum("qhgd,khd->hgqk", query_grid, key_heads, preferred_element_type=jnp.float32)
        * inv_root
    )
    visible = (key_pos[None, :] >= seg_start[:, None]) & (key_pos[None, :] <= token_pos[:, None])
    score = jnp.where(visible[None, None], score, masked)
    top = jnp.max(score, axis=-1, keepdims=True)
    weights = jnp.where(visible[None, None], jnp.exp(score - top), 0.0)
    denom = jnp.sum(weights, axis=-1)
    summed = jnp.einsum(
        "hgqk,khd->hgqd",
        weights.astype(jnp.bfloat16),
        value_heads,
        preferred_element_type=jnp.float32,
    )
    attn = summed / denom[..., None]
    attn = jnp.transpose(attn, (2, 0, 1, 3)).reshape(tokens, q_cols).astype(jnp.bfloat16)
    part = jnp.dot(attn, w_out, preferred_element_type=jnp.float32).astype(jnp.bfloat16)
    nyhi = lax.axis_size("yhi")
    ncore = lax.axis_size("core")
    chunk = tokens // (nyhi * ncore)
    part = part.reshape(nyhi, ncore, chunk, -1).transpose(1, 0, 2, 3)
    part = lax.all_to_all(part, "core", 0, 0, tiled=True)
    part = jnp.sum(part.astype(jnp.float32), axis=0).astype(jnp.bfloat16)
    part = lax.all_to_all(part, "yhi", 0, 0, tiled=True)
    mixed = jnp.sum(part.astype(jnp.float32), axis=0).astype(jnp.bfloat16)
    return (mixed, key_flat, value_flat)


def solution(mesh):
    devices = mesh.devices
    nseq, nten = devices.shape
    nz = len({d.coords[2] for d in devices[:, 0]})
    nx = len({d.coords[0] for d in devices[:, 0]})
    ncore = len({d.core_on_chip for d in devices[0, :]})
    split = Mesh(devices.reshape(nz, nx, nseq // (nz * nx), nten // ncore, ncore), SEQ + TEN)
    seq, ten = SEQ, TEN
    placed = (
        P(seq, ten),
        P(),
        P(None, ten),
        P(None, ten),
        P(None, ten),
        P(ten, None),
        P(),
        P(),
        P(),
    )
    return jax.shard_map(
        on_device,
        mesh=split,
        in_specs=placed,
        out_specs=(P(seq + ten, None), P(seq, ten), P(seq, ten)),
        check_vma=False,
    )
```

```python
import math

import jax
import jax.numpy as jnp
from jax import lax
from jax.sharding import Mesh
from jax.sharding import PartitionSpec as P

rope_base = 1000000.0
norm_eps = 1e-06
masked = -1e30
max_len = 6144

SEQ = ("z", "x", "ylo")
TEN = ("yhi", "core")


def prompt_starts(lengths, token_pos):
    ends = jnp.cumsum(lengths)
    starts = ends - lengths
    before = (ends[None, :] <= token_pos[:, None]).astype(jnp.int32)
    segment = jnp.sum(before, axis=1)
    onehot = segment[:, None] == jnp.arange(lengths.shape[0], dtype=jnp.int32)[None, :]
    return jnp.sum(jnp.where(onehot, starts[None, :], 0), axis=1)


def head_norm_rope(values, gain, rel_pos):
    width = values.shape[-1]
    half = width // 2
    mean_sq = jnp.mean(values * values, axis=-1, keepdims=True)
    normed = values * lax.rsqrt(mean_sq + norm_eps) * gain
    freq = rope_base ** (-jnp.arange(half, dtype=jnp.float32) * 2.0 / width)
    angle = rel_pos.astype(jnp.float32)[:, None] * freq[None, :]
    cosine = jnp.cos(angle)[:, None, :]
    sine = jnp.sin(angle)[:, None, :]
    first = normed[..., :half]
    second = normed[..., half:]
    return jnp.concatenate(
        [first * cosine - second * sine, second * cosine + first * sine], axis=-1
    )


def ring_gather(piece, inner, name, stride):
    n = lax.axis_size(name)
    c = lax.axis_index(name)
    cw = [(i, (i + 1) % n) for i in range(n)]
    ccw = [(i, (i - 1) % n) for i in range(n)]
    pieces, ids = [piece], [c * stride + inner]
    a = b = piece
    for s in range(1, (n - 1) // 2 + 1):
        a = lax.ppermute(a, name, cw)
        b = lax.ppermute(b, name, ccw)
        pieces += [a, b]
        ids += [((c - s) % n) * stride + inner, ((c + s) % n) * stride + inner]
    if n % 2 == 0:
        far = ((c + n // 2) % n) * stride
        m = piece.shape[0]
        if m % 2 == 0:
            pieces += [lax.ppermute(a[: m // 2], name, cw), lax.ppermute(b[m // 2 :], name, ccw)]
            ids += [far + inner[: m // 2], far + inner[m // 2 :]]
        else:
            pieces += [lax.ppermute(a, name, cw)]
            ids += [far + inner]
    return jnp.concatenate(pieces, axis=0), jnp.concatenate(ids, axis=0)


def on_device(hidden_in, norm_gain, w_query, w_key, w_value, w_out, q_gain, k_gain, lengths):
    tokens = hidden_in.shape[0]
    width = w_query.shape[0]
    head_dim = q_gain.shape[0]
    q_cols = w_query.shape[1]
    kv_cols = w_key.shape[1]
    kv_local = kv_cols // head_dim
    group = q_cols // kv_cols
    combined = jnp.concatenate([w_query, w_key, w_value], axis=1)
    piece = lax.all_gather(hidden_in, TEN, axis=1, tiled=True)
    wide = piece.astype(jnp.float32)
    scaled = (wide * norm_gain[None, :]).astype(jnp.bfloat16)
    acc = jnp.dot(scaled, combined, preferred_element_type=jnp.float32)
    sumsq = jnp.sum(wide * wide, axis=1)
    proj = acc * lax.rsqrt(sumsq / width + norm_eps)[:, None]
    block_index = lax.axis_index(SEQ)
    token_pos = block_index * tokens + jnp.arange(tokens, dtype=jnp.int32)
    seg_start = prompt_starts(lengths, token_pos)
    rel_pos = token_pos - seg_start
    queries = head_norm_rope(
        proj[:, :q_cols].reshape(tokens, kv_local * group, head_dim), q_gain, rel_pos
    ).astype(jnp.bfloat16)
    keys = head_norm_rope(
        proj[:, q_cols : q_cols + kv_cols].reshape(tokens, kv_local, head_dim), k_gain, rel_pos
    ).astype(jnp.bfloat16)
    key_flat = keys.reshape(tokens, kv_cols)
    value_flat = proj[:, q_cols + kv_cols :].astype(jnp.bfloat16)

    nx, nlo = lax.axis_size("x"), lax.axis_size("ylo")
    piece = jnp.concatenate([key_flat, value_flat], axis=1)[None]
    block_ids = jnp.zeros((1,), jnp.int32)
    plane = nx * nlo
    piece = lax.all_to_all(jnp.broadcast_to(piece, (plane,) + piece.shape[1:]), ("x", "ylo"), 0, 0, tiled=True)
    block_ids = jnp.arange(plane, dtype=jnp.int32)
    piece, block_ids = ring_gather(piece, block_ids, "z", nx * nlo)
    span = piece.shape[0] * tokens
    kv_all = piece.reshape(span, 2 * kv_cols)
    key_pos = (block_ids[:, None] * tokens + jnp.arange(tokens, dtype=jnp.int32)[None, :]).reshape(span)
    key_heads = kv_all[:, :kv_cols].reshape(span, kv_local, head_dim)
    value_heads = kv_all[:, kv_cols:].reshape(span, kv_local, head_dim)
    query_grid = queries.reshape(tokens, kv_local, group, head_dim)
    inv_root = 1.0 / math.sqrt(head_dim)
    score = (
        jnp.einsum("qhgd,khd->hgqk", query_grid, key_heads, preferred_element_type=jnp.float32)
        * inv_root
    )
    visible = (key_pos[None, :] >= seg_start[:, None]) & (key_pos[None, :] <= token_pos[:, None])
    score = jnp.where(visible[None, None], score, masked)
    top = jnp.max(score, axis=-1, keepdims=True)
    weights = jnp.where(visible[None, None], jnp.exp(score - top), 0.0)
    denom = jnp.sum(weights, axis=-1)
    summed = jnp.einsum(
        "hgqk,khd->hgqd",
        weights.astype(jnp.bfloat16),
        value_heads,
        preferred_element_type=jnp.float32,
    )
    attn = summed / denom[..., None]
    attn = jnp.transpose(attn, (2, 0, 1, 3)).reshape(tokens, q_cols).astype(jnp.bfloat16)
    part = jnp.dot(attn, w_out, preferred_element_type=jnp.float32).astype(jnp.bfloat16)
    nten = lax.axis_size(TEN)
    part = part.reshape(nten, tokens // nten, -1)
    part = lax.all_to_all(part, TEN, 0, 0, tiled=True)
    mixed = jnp.sum(part.astype(jnp.float32), axis=0).astype(jnp.bfloat16)
    return (mixed, key_flat, value_flat)


def solution(mesh):
    devices = mesh.devices
    nseq, nten = devices.shape
    nz = len({d.coords[2] for d in devices[:, 0]})
    nx = len({d.coords[0] for d in devices[:, 0]})
    ncore = len({d.core_on_chip for d in devices[0, :]})
    split = Mesh(devices.reshape(nz, nx, nseq // (nz * nx), nten // ncore, ncore), SEQ + TEN)
    seq, ten = SEQ, TEN
    placed = (
        P(seq, ten),
        P(),
        P(None, ten),
        P(None, ten),
        P(None, ten),
        P(ten, None),
        P(),
        P(),
        P(),
    )
    return jax.shard_map(
        on_device,
        mesh=split,
        in_specs=placed,
        out_specs=(P(seq + ten, None), P(seq, ten), P(seq, ten)),
        check_vma=False,
    )
```

```python
import math

import jax
import jax.numpy as jnp
from jax import lax
from jax.sharding import Mesh
from jax.sharding import PartitionSpec as P

rope_base = 1000000.0
norm_eps = 1e-06
masked = -1e30
max_len = 6144

SEQ = ("z", "x", "ylo")
TEN = ("yhi", "core")


def prompt_starts(lengths, token_pos):
    ends = jnp.cumsum(lengths)
    starts = ends - lengths
    before = (ends[None, :] <= token_pos[:, None]).astype(jnp.int32)
    segment = jnp.sum(before, axis=1)
    onehot = segment[:, None] == jnp.arange(lengths.shape[0], dtype=jnp.int32)[None, :]
    return jnp.sum(jnp.where(onehot, starts[None, :], 0), axis=1)


def head_norm_rope(values, gain, rel_pos):
    width = values.shape[-1]
    half = width // 2
    mean_sq = jnp.mean(values * values, axis=-1, keepdims=True)
    normed = values * lax.rsqrt(mean_sq + norm_eps) * gain
    freq = rope_base ** (-jnp.arange(half, dtype=jnp.float32) * 2.0 / width)
    angle = rel_pos.astype(jnp.float32)[:, None] * freq[None, :]
    cosine = jnp.cos(angle)[:, None, :]
    sine = jnp.sin(angle)[:, None, :]
    first = normed[..., :half]
    second = normed[..., half:]
    return jnp.concatenate(
        [first * cosine - second * sine, second * cosine + first * sine], axis=-1
    )


def ring_gather(piece, inner, name, stride):
    n = lax.axis_size(name)
    c = lax.axis_index(name)
    cw = [(i, (i + 1) % n) for i in range(n)]
    ccw = [(i, (i - 1) % n) for i in range(n)]
    pieces, ids = [piece], [c * stride + inner]
    a = b = piece
    for s in range(1, (n - 1) // 2 + 1):
        a = lax.ppermute(a, name, cw)
        b = lax.ppermute(b, name, ccw)
        pieces += [a, b]
        ids += [((c - s) % n) * stride + inner, ((c + s) % n) * stride + inner]
    if n % 2 == 0:
        far = ((c + n // 2) % n) * stride
        m = piece.shape[0]
        if m % 2 == 0:
            pieces += [lax.ppermute(a[: m // 2], name, cw), lax.ppermute(b[m // 2 :], name, ccw)]
            ids += [far + inner[: m // 2], far + inner[m // 2 :]]
        else:
            pieces += [lax.ppermute(a, name, cw)]
            ids += [far + inner]
    return jnp.concatenate(pieces, axis=0), jnp.concatenate(ids, axis=0)


def on_device(hidden_in, norm_gain, w_query, w_key, w_value, w_out, q_gain, k_gain, lengths):
    tokens = hidden_in.shape[0]
    width = w_query.shape[0]
    head_dim = q_gain.shape[0]
    q_cols = w_query.shape[1]
    kv_cols = w_key.shape[1]
    kv_local = kv_cols // head_dim
    group = q_cols // kv_cols
    combined = jnp.concatenate([w_query, w_key, w_value], axis=1)
    piece = lax.all_gather(hidden_in, "core", axis=0, tiled=False)
    piece = lax.all_gather(piece, "yhi", axis=0, tiled=False)
    piece = jnp.moveaxis(piece.reshape(-1, *hidden_in.shape), 0, 1).reshape(hidden_in.shape[0], -1)
    wide = piece.astype(jnp.float32)
    scaled = (wide * norm_gain[None, :]).astype(jnp.bfloat16)
    acc = jnp.dot(scaled, combined, preferred_element_type=jnp.float32)
    sumsq = jnp.sum(wide * wide, axis=1)
    proj = acc * lax.rsqrt(sumsq / width + norm_eps)[:, None]
    block_index = lax.axis_index(SEQ)
    token_pos = block_index * tokens + jnp.arange(tokens, dtype=jnp.int32)
    seg_start = prompt_starts(lengths, token_pos)
    rel_pos = token_pos - seg_start
    queries = head_norm_rope(
        proj[:, :q_cols].reshape(tokens, kv_local * group, head_dim), q_gain, rel_pos
    ).astype(jnp.bfloat16)
    keys = head_norm_rope(
        proj[:, q_cols : q_cols + kv_cols].reshape(tokens, kv_local, head_dim), k_gain, rel_pos
    ).astype(jnp.bfloat16)
    key_flat = keys.reshape(tokens, kv_cols)
    value_flat = proj[:, q_cols + kv_cols :].astype(jnp.bfloat16)

    nx, nlo = lax.axis_size("x"), lax.axis_size("ylo")
    piece = jnp.concatenate([key_flat, value_flat], axis=1)[None]
    block_ids = jnp.zeros((1,), jnp.int32)
    plane = nx * nlo
    piece = lax.all_to_all(jnp.broadcast_to(piece, (plane,) + piece.shape[1:]), ("x", "ylo"), 0, 0, tiled=True)
    block_ids = jnp.arange(plane, dtype=jnp.int32)
    piece, block_ids = ring_gather(piece, block_ids, "z", nx * nlo)
    span = piece.shape[0] * tokens
    kv_all = piece.reshape(span, 2 * kv_cols)
    key_pos = (block_ids[:, None] * tokens + jnp.arange(tokens, dtype=jnp.int32)[None, :]).reshape(span)
    key_heads = kv_all[:, :kv_cols].reshape(span, kv_local, head_dim)
    value_heads = kv_all[:, kv_cols:].reshape(span, kv_local, head_dim)
    query_grid = queries.reshape(tokens, kv_local, group, head_dim)
    inv_root = 1.0 / math.sqrt(head_dim)
    score = (
        jnp.einsum("qhgd,khd->hgqk", query_grid, key_heads, preferred_element_type=jnp.float32)
        * inv_root
    )
    visible = (key_pos[None, :] >= seg_start[:, None]) & (key_pos[None, :] <= token_pos[:, None])
    score = jnp.where(visible[None, None], score, masked)
    top = jnp.max(score, axis=-1, keepdims=True)
    weights = jnp.where(visible[None, None], jnp.exp(score - top), 0.0)
    denom = jnp.sum(weights, axis=-1)
    summed = jnp.einsum(
        "hgqk,khd->hgqd",
        weights.astype(jnp.bfloat16),
        value_heads,
        preferred_element_type=jnp.float32,
    )
    attn = summed / denom[..., None]
    attn = jnp.transpose(attn, (2, 0, 1, 3)).reshape(tokens, q_cols).astype(jnp.bfloat16)
    part = jnp.dot(attn, w_out, preferred_element_type=jnp.float32).astype(jnp.bfloat16)
    nyhi = lax.axis_size("yhi")
    ncore = lax.axis_size("core")
    chunk = tokens // (nyhi * ncore)
    part = part.reshape(nyhi, ncore, chunk, -1).transpose(1, 0, 2, 3)
    part = lax.all_to_all(part, "core", 0, 0, tiled=True)
    part = jnp.sum(part.astype(jnp.float32), axis=0).astype(jnp.bfloat16)
    part = lax.all_to_all(part, "yhi", 0, 0, tiled=True)
    mixed = jnp.sum(part.astype(jnp.float32), axis=0).astype(jnp.bfloat16)
    return (mixed, key_flat, value_flat)


def solution(mesh):
    devices = mesh.devices
    nseq, nten = devices.shape
    nz = len({d.coords[2] for d in devices[:, 0]})
    nx = len({d.coords[0] for d in devices[:, 0]})
    ncore = len({d.core_on_chip for d in devices[0, :]})
    split = Mesh(devices.reshape(nz, nx, nseq // (nz * nx), nten // ncore, ncore), SEQ + TEN)
    seq, ten = SEQ, TEN
    placed = (
        P(seq, ten),
        P(),
        P(None, ten),
        P(None, ten),
        P(None, ten),
        P(ten, None),
        P(),
        P(),
        P(),
    )
    return jax.shard_map(
        on_device,
        mesh=split,
        in_specs=placed,
        out_specs=(P(seq + ten, None), P(seq, ten), P(seq, ten)),
        check_vma=False,
    )
```

```python
import math

import jax
import jax.numpy as jnp
from jax import lax
from jax.sharding import Mesh
from jax.sharding import PartitionSpec as P

rope_base = 1000000.0
norm_eps = 1e-06
masked = -1e30
max_len = 6144

SEQ = ("z", "x", "ylo")
TEN = ("yhi", "core")


def prompt_starts(lengths, token_pos):
    ends = jnp.cumsum(lengths)
    starts = ends - lengths
    before = (ends[None, :] <= token_pos[:, None]).astype(jnp.int32)
    segment = jnp.sum(before, axis=1)
    onehot = segment[:, None] == jnp.arange(lengths.shape[0], dtype=jnp.int32)[None, :]
    return jnp.sum(jnp.where(onehot, starts[None, :], 0), axis=1)


def head_norm_rope(values, gain, rel_pos):
    width = values.shape[-1]
    half = width // 2
    mean_sq = jnp.mean(values * values, axis=-1, keepdims=True)
    normed = values * lax.rsqrt(mean_sq + norm_eps) * gain
    freq = rope_base ** (-jnp.arange(half, dtype=jnp.float32) * 2.0 / width)
    angle = rel_pos.astype(jnp.float32)[:, None] * freq[None, :]
    cosine = jnp.cos(angle)[:, None, :]
    sine = jnp.sin(angle)[:, None, :]
    first = normed[..., :half]
    second = normed[..., half:]
    return jnp.concatenate(
        [first * cosine - second * sine, second * cosine + first * sine], axis=-1
    )


def ring_gather(piece, inner, name, stride):
    n = lax.axis_size(name)
    c = lax.axis_index(name)
    cw = [(i, (i + 1) % n) for i in range(n)]
    ccw = [(i, (i - 1) % n) for i in range(n)]
    pieces, ids = [piece], [c * stride + inner]
    a = b = piece
    for s in range(1, (n - 1) // 2 + 1):
        a = lax.ppermute(a, name, cw)
        b = lax.ppermute(b, name, ccw)
        pieces += [a, b]
        ids += [((c - s) % n) * stride + inner, ((c + s) % n) * stride + inner]
    if n % 2 == 0:
        far = ((c + n // 2) % n) * stride
        m = piece.shape[0]
        if m % 2 == 0:
            pieces += [lax.ppermute(a[: m // 2], name, cw), lax.ppermute(b[m // 2 :], name, ccw)]
            ids += [far + inner[: m // 2], far + inner[m // 2 :]]
        else:
            pieces += [lax.ppermute(a, name, cw)]
            ids += [far + inner]
    return jnp.concatenate(pieces, axis=0), jnp.concatenate(ids, axis=0)


def on_device(hidden_in, norm_gain, w_query, w_key, w_value, w_out, q_gain, k_gain, lengths):
    tokens = hidden_in.shape[0]
    width = w_query.shape[0]
    head_dim = q_gain.shape[0]
    q_cols = w_query.shape[1]
    kv_cols = w_key.shape[1]
    kv_local = kv_cols // head_dim
    group = q_cols // kv_cols
    combined = jnp.concatenate([w_query, w_key, w_value], axis=1)
    piece = lax.all_gather(hidden_in, TEN, axis=1, tiled=True)
    wide = piece.astype(jnp.float32)
    scaled = (wide * norm_gain[None, :]).astype(jnp.bfloat16)
    acc = jnp.dot(scaled, combined, preferred_element_type=jnp.float32)
    sumsq = jnp.sum(wide * wide, axis=1)
    proj = acc * lax.rsqrt(sumsq / width + norm_eps)[:, None]
    block_index = lax.axis_index(SEQ)
    token_pos = block_index * tokens + jnp.arange(tokens, dtype=jnp.int32)
    seg_start = prompt_starts(lengths, token_pos)
    rel_pos = token_pos - seg_start
    queries = head_norm_rope(
        proj[:, :q_cols].reshape(tokens, kv_local * group, head_dim), q_gain, rel_pos
    ).astype(jnp.bfloat16)
    keys = head_norm_rope(
        proj[:, q_cols : q_cols + kv_cols].reshape(tokens, kv_local, head_dim), k_gain, rel_pos
    ).astype(jnp.bfloat16)
    key_flat = keys.reshape(tokens, kv_cols)
    value_flat = proj[:, q_cols + kv_cols :].astype(jnp.bfloat16)

    nseq = lax.axis_size(SEQ)
    piece = jnp.concatenate([key_flat, value_flat], axis=1)[None]
    piece = lax.all_to_all(jnp.broadcast_to(piece, (nseq,) + piece.shape[1:]), SEQ, 0, 0, tiled=True)
    block_ids = jnp.arange(nseq, dtype=jnp.int32)
    span = piece.shape[0] * tokens
    kv_all = piece.reshape(span, 2 * kv_cols)
    key_pos = (block_ids[:, None] * tokens + jnp.arange(tokens, dtype=jnp.int32)[None, :]).reshape(span)
    key_heads = kv_all[:, :kv_cols].reshape(span, kv_local, head_dim)
    value_heads = kv_all[:, kv_cols:].reshape(span, kv_local, head_dim)
    query_grid = queries.reshape(tokens, kv_local, group, head_dim)
    inv_root = 1.0 / math.sqrt(head_dim)
    score = (
        jnp.einsum("qhgd,khd->hgqk", query_grid, key_heads, preferred_element_type=jnp.float32)
        * inv_root
    )
    visible = (key_pos[None, :] >= seg_start[:, None]) & (key_pos[None, :] <= token_pos[:, None])
    score = jnp.where(visible[None, None], score, masked)
    top = jnp.max(score, axis=-1, keepdims=True)
    weights = jnp.where(visible[None, None], jnp.exp(score - top), 0.0)
    denom = jnp.sum(weights, axis=-1)
    summed = jnp.einsum(
        "hgqk,khd->hgqd",
        weights.astype(jnp.bfloat16),
        value_heads,
        preferred_element_type=jnp.float32,
    )
    attn = summed / denom[..., None]
    attn = jnp.transpose(attn, (2, 0, 1, 3)).reshape(tokens, q_cols).astype(jnp.bfloat16)
    part = jnp.dot(attn, w_out, preferred_element_type=jnp.float32).astype(jnp.bfloat16)
    nyhi = lax.axis_size("yhi")
    ncore = lax.axis_size("core")
    chunk = tokens // (nyhi * ncore)
    part = part.reshape(nyhi, ncore, chunk, -1).transpose(1, 0, 2, 3)
    part = lax.all_to_all(part, "core", 0, 0, tiled=True)
    part = jnp.sum(part.astype(jnp.float32), axis=0).astype(jnp.bfloat16)
    part = lax.all_to_all(part, "yhi", 0, 0, tiled=True)
    mixed = jnp.sum(part.astype(jnp.float32), axis=0).astype(jnp.bfloat16)
    return (mixed, key_flat, value_flat)


def solution(mesh):
    devices = mesh.devices
    nseq, nten = devices.shape
    nz = len({d.coords[2] for d in devices[:, 0]})
    nx = len({d.coords[0] for d in devices[:, 0]})
    ncore = len({d.core_on_chip for d in devices[0, :]})
    split = Mesh(devices.reshape(nz, nx, nseq // (nz * nx), nten // ncore, ncore), SEQ + TEN)
    seq, ten = SEQ, TEN
    placed = (
        P(seq, ten),
        P(),
        P(None, ten),
        P(None, ten),
        P(None, ten),
        P(ten, None),
        P(),
        P(),
        P(),
    )
    return jax.shard_map(
        on_device,
        mesh=split,
        in_specs=placed,
        out_specs=(P(seq + ten, None), P(seq, ten), P(seq, ten)),
        check_vma=False,
    )
```

```python
import math

import jax
import jax.numpy as jnp
from jax import lax
from jax.sharding import Mesh
from jax.sharding import PartitionSpec as P

rope_base = 1000000.0
norm_eps = 1e-06
masked = -1e30
max_len = 6144

SEQ = ("z", "x", "ylo")
TEN = ("yhi", "core")


def prompt_starts(lengths, token_pos):
    ends = jnp.cumsum(lengths)
    starts = ends - lengths
    before = (ends[None, :] <= token_pos[:, None]).astype(jnp.int32)
    segment = jnp.sum(before, axis=1)
    onehot = segment[:, None] == jnp.arange(lengths.shape[0], dtype=jnp.int32)[None, :]
    return jnp.sum(jnp.where(onehot, starts[None, :], 0), axis=1)


def head_norm_rope(values, gain, rel_pos):
    width = values.shape[-1]
    half = width // 2
    mean_sq = jnp.mean(values * values, axis=-1, keepdims=True)
    normed = values * lax.rsqrt(mean_sq + norm_eps) * gain
    freq = rope_base ** (-jnp.arange(half, dtype=jnp.float32) * 2.0 / width)
    angle = rel_pos.astype(jnp.float32)[:, None] * freq[None, :]
    cosine = jnp.cos(angle)[:, None, :]
    sine = jnp.sin(angle)[:, None, :]
    first = normed[..., :half]
    second = normed[..., half:]
    return jnp.concatenate(
        [first * cosine - second * sine, second * cosine + first * sine], axis=-1
    )


def ring_gather(piece, inner, name, stride):
    n = lax.axis_size(name)
    c = lax.axis_index(name)
    cw = [(i, (i + 1) % n) for i in range(n)]
    ccw = [(i, (i - 1) % n) for i in range(n)]
    pieces, ids = [piece], [c * stride + inner]
    a = b = piece
    for s in range(1, (n - 1) // 2 + 1):
        a = lax.ppermute(a, name, cw)
        b = lax.ppermute(b, name, ccw)
        pieces += [a, b]
        ids += [((c - s) % n) * stride + inner, ((c + s) % n) * stride + inner]
    if n % 2 == 0:
        far = ((c + n // 2) % n) * stride
        m = piece.shape[0]
        if m % 2 == 0:
            pieces += [lax.ppermute(a[: m // 2], name, cw), lax.ppermute(b[m // 2 :], name, ccw)]
            ids += [far + inner[: m // 2], far + inner[m // 2 :]]
        else:
            pieces += [lax.ppermute(a, name, cw)]
            ids += [far + inner]
    return jnp.concatenate(pieces, axis=0), jnp.concatenate(ids, axis=0)


def on_device(hidden_in, norm_gain, w_query, w_key, w_value, w_out, q_gain, k_gain, lengths):
    tokens = hidden_in.shape[0]
    width = w_query.shape[0]
    head_dim = q_gain.shape[0]
    q_cols = w_query.shape[1]
    kv_cols = w_key.shape[1]
    kv_local = kv_cols // head_dim
    group = q_cols // kv_cols
    combined = jnp.concatenate([w_query, w_key, w_value], axis=1)
    piece = lax.all_gather(hidden_in, TEN, axis=1, tiled=True)
    wide = piece.astype(jnp.float32)
    scaled = (wide * norm_gain[None, :]).astype(jnp.bfloat16)
    acc = jnp.dot(scaled, combined, preferred_element_type=jnp.float32)
    sumsq = jnp.sum(wide * wide, axis=1)
    proj = acc * lax.rsqrt(sumsq / width + norm_eps)[:, None]
    block_index = lax.axis_index(SEQ)
    token_pos = block_index * tokens + jnp.arange(tokens, dtype=jnp.int32)
    seg_start = prompt_starts(lengths, token_pos)
    rel_pos = token_pos - seg_start
    queries = head_norm_rope(
        proj[:, :q_cols].reshape(tokens, kv_local * group, head_dim), q_gain, rel_pos
    ).astype(jnp.bfloat16)
    keys = head_norm_rope(
        proj[:, q_cols : q_cols + kv_cols].reshape(tokens, kv_local, head_dim), k_gain, rel_pos
    ).astype(jnp.bfloat16)
    key_flat = keys.reshape(tokens, kv_cols)
    value_flat = proj[:, q_cols + kv_cols :].astype(jnp.bfloat16)

    nx, nlo = lax.axis_size("x"), lax.axis_size("ylo")
    piece = jnp.concatenate([key_flat, value_flat], axis=1)[None]
    block_ids = jnp.zeros((1,), jnp.int32)
    plane = nx * nlo
    piece = lax.all_to_all(jnp.broadcast_to(piece, (plane,) + piece.shape[1:]), ("x", "ylo"), 0, 0, tiled=True)
    block_ids = jnp.arange(plane, dtype=jnp.int32)
    nz = lax.axis_size("z")
    kz = lax.all_gather(piece[..., :kv_cols], "z", axis=0, tiled=True)
    vz, vids = ring_gather(piece[..., kv_cols:], block_ids, "z", plane)
    slot_of = jnp.zeros((nz,), jnp.int32).at[vids[::plane] // plane].set(jnp.arange(nz, dtype=jnp.int32))
    vz = jnp.take(vz.reshape(nz, plane, tokens, kv_cols), slot_of, axis=0)
    span = nz * plane * tokens
    key_pos = jnp.arange(span, dtype=jnp.int32)
    key_heads = kz.reshape(span, kv_local, head_dim)
    value_heads = vz.reshape(span, kv_local, head_dim)
    query_grid = queries.reshape(tokens, kv_local, group, head_dim)
    inv_root = 1.0 / math.sqrt(head_dim)
    score = (
        jnp.einsum("qhgd,khd->hgqk", query_grid, key_heads, preferred_element_type=jnp.float32)
        * inv_root
    )
    visible = (key_pos[None, :] >= seg_start[:, None]) & (key_pos[None, :] <= token_pos[:, None])
    score = jnp.where(visible[None, None], score, masked)
    top = jnp.max(score, axis=-1, keepdims=True)
    weights = jnp.where(visible[None, None], jnp.exp(score - top), 0.0)
    denom = jnp.sum(weights, axis=-1)
    summed = jnp.einsum(
        "hgqk,khd->hgqd",
        weights.astype(jnp.bfloat16),
        value_heads,
        preferred_element_type=jnp.float32,
    )
    attn = summed / denom[..., None]
    attn = jnp.transpose(attn, (2, 0, 1, 3)).reshape(tokens, q_cols).astype(jnp.bfloat16)
    part = jnp.dot(attn, w_out, preferred_element_type=jnp.float32).astype(jnp.bfloat16)
    nyhi = lax.axis_size("yhi")
    ncore = lax.axis_size("core")
    chunk = tokens // (nyhi * ncore)
    part = part.reshape(nyhi, ncore, chunk, -1).transpose(1, 0, 2, 3)
    part = lax.all_to_all(part, "core", 0, 0, tiled=True)
    part = jnp.sum(part.astype(jnp.float32), axis=0).astype(jnp.bfloat16)
    part = lax.all_to_all(part, "yhi", 0, 0, tiled=True)
    mixed = jnp.sum(part.astype(jnp.float32), axis=0).astype(jnp.bfloat16)
    return (mixed, key_flat, value_flat)


def solution(mesh):
    devices = mesh.devices
    nseq, nten = devices.shape
    nz = len({d.coords[2] for d in devices[:, 0]})
    nx = len({d.coords[0] for d in devices[:, 0]})
    ncore = len({d.core_on_chip for d in devices[0, :]})
    split = Mesh(devices.reshape(nz, nx, nseq // (nz * nx), nten // ncore, ncore), SEQ + TEN)
    seq, ten = SEQ, TEN
    placed = (
        P(seq, ten),
        P(),
        P(None, ten),
        P(None, ten),
        P(None, ten),
        P(ten, None),
        P(),
        P(),
        P(),
    )
    return jax.shard_map(
        on_device,
        mesh=split,
        in_specs=placed,
        out_specs=(P(seq + ten, None), P(seq, ten), P(seq, ten)),
        check_vma=False,
    )
```

```python
import math

import jax
import jax.numpy as jnp
from jax import lax
from jax.sharding import Mesh
from jax.sharding import PartitionSpec as P

rope_base = 1000000.0
norm_eps = 1e-06
masked = -1e30
max_len = 6144

SEQ = ("z", "x", "ylo")
TEN = ("yhi", "core")


def prompt_starts(lengths, token_pos):
    ends = jnp.cumsum(lengths)
    starts = ends - lengths
    before = (ends[None, :] <= token_pos[:, None]).astype(jnp.int32)
    segment = jnp.sum(before, axis=1)
    onehot = segment[:, None] == jnp.arange(lengths.shape[0], dtype=jnp.int32)[None, :]
    return jnp.sum(jnp.where(onehot, starts[None, :], 0), axis=1)


def head_norm_rope(values, gain, rel_pos):
    width = values.shape[-1]
    half = width // 2
    mean_sq = jnp.mean(values * values, axis=-1, keepdims=True)
    normed = values * lax.rsqrt(mean_sq + norm_eps) * gain
    freq = rope_base ** (-jnp.arange(half, dtype=jnp.float32) * 2.0 / width)
    angle = rel_pos.astype(jnp.float32)[:, None] * freq[None, :]
    cosine = jnp.cos(angle)[:, None, :]
    sine = jnp.sin(angle)[:, None, :]
    first = normed[..., :half]
    second = normed[..., half:]
    return jnp.concatenate(
        [first * cosine - second * sine, second * cosine + first * sine], axis=-1
    )


def ring_pairs(n, k, forward, needed):
    out = []
    for src in range(n):
        if forward:
            start, dst = (src - (k - 1)) % n, (src + 1) % n
            reach = [(start + j) % n for j in range(k, n // 2 + 1)]
        else:
            start, dst = (src + (k - 1)) % n, (src - 1) % n
            reach = [(start - j) % n for j in range(k, n // 2 + 1)]
        if any(needed(start, d) for d in reach):
            out.append((src, dst))
    return out


def ring_gather(piece, inner, name, stride, needed=lambda p, d: True):
    n = lax.axis_size(name)
    c = lax.axis_index(name)
    pieces, ids = [piece], [c * stride + inner]
    a = b = piece
    for s in range(1, (n - 1) // 2 + 1):
        a = lax.ppermute(a, name, ring_pairs(n, s, True, needed))
        b = lax.ppermute(b, name, ring_pairs(n, s, False, needed))
        pieces += [a, b]
        ids += [((c - s) % n) * stride + inner, ((c + s) % n) * stride + inner]
    if n % 2 == 0:
        s = n // 2
        far = ((c + s) % n) * stride
        m = piece.shape[0]
        if m % 2 == 0:
            pieces += [
                lax.ppermute(a[: m // 2], name, ring_pairs(n, s, True, needed)),
                lax.ppermute(b[m // 2 :], name, ring_pairs(n, s, False, needed)),
            ]
            ids += [far + inner[: m // 2], far + inner[m // 2 :]]
        else:
            pieces += [lax.ppermute(a, name, ring_pairs(n, s, True, needed))]
            ids += [far + inner]
    return jnp.concatenate(pieces, axis=0), jnp.concatenate(ids, axis=0)


def on_device(hidden_in, norm_gain, w_query, w_key, w_value, w_out, q_gain, k_gain, lengths):
    tokens = hidden_in.shape[0]
    width = w_query.shape[0]
    head_dim = q_gain.shape[0]
    q_cols = w_query.shape[1]
    kv_cols = w_key.shape[1]
    kv_local = kv_cols // head_dim
    group = q_cols // kv_cols
    combined = jnp.concatenate([w_query, w_key, w_value], axis=1)
    piece = lax.all_gather(hidden_in, TEN, axis=1, tiled=True)
    wide = piece.astype(jnp.float32)
    scaled = (wide * norm_gain[None, :]).astype(jnp.bfloat16)
    acc = jnp.dot(scaled, combined, preferred_element_type=jnp.float32)
    sumsq = jnp.sum(wide * wide, axis=1)
    proj = acc * lax.rsqrt(sumsq / width + norm_eps)[:, None]
    block_index = lax.axis_index(SEQ)
    token_pos = block_index * tokens + jnp.arange(tokens, dtype=jnp.int32)
    seg_start = prompt_starts(lengths, token_pos)
    rel_pos = token_pos - seg_start
    queries = head_norm_rope(
        proj[:, :q_cols].reshape(tokens, kv_local * group, head_dim), q_gain, rel_pos
    ).astype(jnp.bfloat16)
    keys = head_norm_rope(
        proj[:, q_cols : q_cols + kv_cols].reshape(tokens, kv_local, head_dim), k_gain, rel_pos
    ).astype(jnp.bfloat16)
    key_flat = keys.reshape(tokens, kv_cols)
    value_flat = proj[:, q_cols + kv_cols :].astype(jnp.bfloat16)

    nx, nlo = lax.axis_size("x"), lax.axis_size("ylo")
    piece = jnp.concatenate([key_flat, value_flat], axis=1)[None]
    block_ids = jnp.zeros((1,), jnp.int32)
    plane = nx * nlo
    piece = lax.all_to_all(jnp.broadcast_to(piece, (plane,) + piece.shape[1:]), ("x", "ylo"), 0, 0, tiled=True)
    block_ids = jnp.arange(plane, dtype=jnp.int32)
    back = -(-(-(-(max_len - 1) // tokens)) // plane)
    piece, block_ids = ring_gather(piece, block_ids, "z", plane, lambda p, d: 1 <= d - p <= back)
    span = piece.shape[0] * tokens
    kv_all = piece.reshape(span, 2 * kv_cols)
    key_pos = (block_ids[:, None] * tokens + jnp.arange(tokens, dtype=jnp.int32)[None, :]).reshape(span)
    key_heads = kv_all[:, :kv_cols].reshape(span, kv_local, head_dim)
    value_heads = kv_all[:, kv_cols:].reshape(span, kv_local, head_dim)
    query_grid = queries.reshape(tokens, kv_local, group, head_dim)
    inv_root = 1.0 / math.sqrt(head_dim)
    score = (
        jnp.einsum("qhgd,khd->hgqk", query_grid, key_heads, preferred_element_type=jnp.float32)
        * inv_root
    )
    visible = (key_pos[None, :] >= seg_start[:, None]) & (key_pos[None, :] <= token_pos[:, None])
    score = jnp.where(visible[None, None], score, masked)
    top = jnp.max(score, axis=-1, keepdims=True)
    weights = jnp.where(visible[None, None], jnp.exp(score - top), 0.0)
    denom = jnp.sum(weights, axis=-1)
    summed = jnp.einsum(
        "hgqk,khd->hgqd",
        weights.astype(jnp.bfloat16),
        value_heads,
        preferred_element_type=jnp.float32,
    )
    attn = summed / denom[..., None]
    attn = jnp.transpose(attn, (2, 0, 1, 3)).reshape(tokens, q_cols).astype(jnp.bfloat16)
    part = jnp.dot(attn, w_out, preferred_element_type=jnp.float32).astype(jnp.bfloat16)
    nyhi = lax.axis_size("yhi")
    ncore = lax.axis_size("core")
    chunk = tokens // (nyhi * ncore)
    part = part.reshape(nyhi, ncore, chunk, -1).transpose(1, 0, 2, 3)
    part = lax.all_to_all(part, "core", 0, 0, tiled=True)
    part = jnp.sum(part.astype(jnp.float32), axis=0).astype(jnp.bfloat16)
    part = lax.all_to_all(part, "yhi", 0, 0, tiled=True)
    mixed = jnp.sum(part.astype(jnp.float32), axis=0).astype(jnp.bfloat16)
    return (mixed, key_flat, value_flat)


def solution(mesh):
    devices = mesh.devices
    nseq, nten = devices.shape
    nz = len({d.coords[2] for d in devices[:, 0]})
    nx = len({d.coords[0] for d in devices[:, 0]})
    ncore = len({d.core_on_chip for d in devices[0, :]})
    split = Mesh(devices.reshape(nz, nx, nseq // (nz * nx), nten // ncore, ncore), SEQ + TEN)
    seq, ten = SEQ, TEN
    placed = (
        P(seq, ten),
        P(),
        P(None, ten),
        P(None, ten),
        P(None, ten),
        P(ten, None),
        P(),
        P(),
        P(),
    )
    return jax.shard_map(
        on_device,
        mesh=split,
        in_specs=placed,
        out_specs=(P(seq + ten, None), P(seq, ten), P(seq, ten)),
        check_vma=False,
    )
```

```python
import math

import jax
import jax.numpy as jnp
from jax import lax
from jax.sharding import Mesh
from jax.sharding import PartitionSpec as P

rope_base = 1000000.0
norm_eps = 1e-06
masked = -1e30
max_len = 6144

SEQ = ("z", "x", "ylo")
TEN = ("yhi", "core")


def prompt_starts(lengths, token_pos):
    ends = jnp.cumsum(lengths)
    starts = ends - lengths
    before = (ends[None, :] <= token_pos[:, None]).astype(jnp.int32)
    segment = jnp.sum(before, axis=1)
    onehot = segment[:, None] == jnp.arange(lengths.shape[0], dtype=jnp.int32)[None, :]
    return jnp.sum(jnp.where(onehot, starts[None, :], 0), axis=1)


def head_norm_rope(values, gain, rel_pos):
    width = values.shape[-1]
    half = width // 2
    mean_sq = jnp.mean(values * values, axis=-1, keepdims=True)
    normed = values * lax.rsqrt(mean_sq + norm_eps) * gain
    freq = rope_base ** (-jnp.arange(half, dtype=jnp.float32) * 2.0 / width)
    angle = rel_pos.astype(jnp.float32)[:, None] * freq[None, :]
    cosine = jnp.cos(angle)[:, None, :]
    sine = jnp.sin(angle)[:, None, :]
    first = normed[..., :half]
    second = normed[..., half:]
    return jnp.concatenate(
        [first * cosine - second * sine, second * cosine + first * sine], axis=-1
    )


def ring_pairs(n, k, forward, needed):
    out = []
    for src in range(n):
        if forward:
            start, dst = (src - (k - 1)) % n, (src + 1) % n
            reach = [(start + j) % n for j in range(k, n // 2 + 1)]
        else:
            start, dst = (src + (k - 1)) % n, (src - 1) % n
            reach = [(start - j) % n for j in range(k, n // 2 + 1)]
        if any(needed(start, d) for d in reach):
            out.append((src, dst))
    return out


def ring_gather(piece, inner, name, stride, needed=lambda p, d: True):
    n = lax.axis_size(name)
    c = lax.axis_index(name)
    pieces, ids = [piece], [c * stride + inner]
    a = b = piece
    if n % 2 == 0 and n >= 4:
        last = n // 2 - 1
        held = a
        for s in range(1, last + 1):
            if s == last:
                hop2 = [(src, (src + 2) % n) for src in range(n) if needed((src - (last - 1)) % n, (src + 2) % n)]
                pieces.append(lax.ppermute(held, name, hop2))
                ids.append(((c + n // 2) % n) * stride + inner)
            a = lax.ppermute(a, name, ring_pairs(n, s, True, needed))
            b = lax.ppermute(b, name, ring_pairs(n, s, False, needed))
            held = a
            pieces += [a, b]
            ids += [((c - s) % n) * stride + inner, ((c + s) % n) * stride + inner]
        return jnp.concatenate(pieces, axis=0), jnp.concatenate(ids, axis=0)
    for s in range(1, (n - 1) // 2 + 1):
        a = lax.ppermute(a, name, ring_pairs(n, s, True, needed))
        b = lax.ppermute(b, name, ring_pairs(n, s, False, needed))
        pieces += [a, b]
        ids += [((c - s) % n) * stride + inner, ((c + s) % n) * stride + inner]
    if n % 2 == 0:
        s = n // 2
        far = ((c + s) % n) * stride
        m = piece.shape[0]
        if m % 2 == 0:
            pieces += [
                lax.ppermute(a[: m // 2], name, ring_pairs(n, s, True, needed)),
                lax.ppermute(b[m // 2 :], name, ring_pairs(n, s, False, needed)),
            ]
            ids += [far + inner[: m // 2], far + inner[m // 2 :]]
        else:
            pieces += [lax.ppermute(a, name, ring_pairs(n, s, True, needed))]
            ids += [far + inner]
    return jnp.concatenate(pieces, axis=0), jnp.concatenate(ids, axis=0)


def on_device(hidden_in, norm_gain, w_query, w_key, w_value, w_out, q_gain, k_gain, lengths):
    tokens = hidden_in.shape[0]
    width = w_query.shape[0]
    head_dim = q_gain.shape[0]
    q_cols = w_query.shape[1]
    kv_cols = w_key.shape[1]
    kv_local = kv_cols // head_dim
    group = q_cols // kv_cols
    combined = jnp.concatenate([w_query, w_key, w_value], axis=1)
    piece = lax.all_gather(hidden_in, TEN, axis=1, tiled=True)
    wide = piece.astype(jnp.float32)
    scaled = (wide * norm_gain[None, :]).astype(jnp.bfloat16)
    acc = jnp.dot(scaled, combined, preferred_element_type=jnp.float32)
    sumsq = jnp.sum(wide * wide, axis=1)
    proj = acc * lax.rsqrt(sumsq / width + norm_eps)[:, None]
    block_index = lax.axis_index(SEQ)
    token_pos = block_index * tokens + jnp.arange(tokens, dtype=jnp.int32)
    seg_start = prompt_starts(lengths, token_pos)
    rel_pos = token_pos - seg_start
    queries = head_norm_rope(
        proj[:, :q_cols].reshape(tokens, kv_local * group, head_dim), q_gain, rel_pos
    ).astype(jnp.bfloat16)
    keys = head_norm_rope(
        proj[:, q_cols : q_cols + kv_cols].reshape(tokens, kv_local, head_dim), k_gain, rel_pos
    ).astype(jnp.bfloat16)
    key_flat = keys.reshape(tokens, kv_cols)
    value_flat = proj[:, q_cols + kv_cols :].astype(jnp.bfloat16)

    nx, nlo = lax.axis_size("x"), lax.axis_size("ylo")
    piece = jnp.concatenate([key_flat, value_flat], axis=1)[None]
    block_ids = jnp.zeros((1,), jnp.int32)
    plane = nx * nlo
    piece = lax.all_to_all(jnp.broadcast_to(piece, (plane,) + piece.shape[1:]), ("x", "ylo"), 0, 0, tiled=True)
    block_ids = jnp.arange(plane, dtype=jnp.int32)
    back = -(-(-(-(max_len - 1) // tokens)) // plane)
    piece, block_ids = ring_gather(piece, block_ids, "z", plane, lambda p, d: 1 <= d - p <= back)
    span = piece.shape[0] * tokens
    kv_all = piece.reshape(span, 2 * kv_cols)
    key_pos = (block_ids[:, None] * tokens + jnp.arange(tokens, dtype=jnp.int32)[None, :]).reshape(span)
    key_heads = kv_all[:, :kv_cols].reshape(span, kv_local, head_dim)
    value_heads = kv_all[:, kv_cols:].reshape(span, kv_local, head_dim)
    query_grid = queries.reshape(tokens, kv_local, group, head_dim)
    inv_root = 1.0 / math.sqrt(head_dim)
    score = (
        jnp.einsum("qhgd,khd->hgqk", query_grid, key_heads, preferred_element_type=jnp.float32)
        * inv_root
    )
    visible = (key_pos[None, :] >= seg_start[:, None]) & (key_pos[None, :] <= token_pos[:, None])
    score = jnp.where(visible[None, None], score, masked)
    top = jnp.max(score, axis=-1, keepdims=True)
    weights = jnp.where(visible[None, None], jnp.exp(score - top), 0.0)
    denom = jnp.sum(weights, axis=-1)
    summed = jnp.einsum(
        "hgqk,khd->hgqd",
        weights.astype(jnp.bfloat16),
        value_heads,
        preferred_element_type=jnp.float32,
    )
    attn = summed / denom[..., None]
    attn = jnp.transpose(attn, (2, 0, 1, 3)).reshape(tokens, q_cols).astype(jnp.bfloat16)
    part = jnp.dot(attn, w_out, preferred_element_type=jnp.float32).astype(jnp.bfloat16)
    nyhi = lax.axis_size("yhi")
    ncore = lax.axis_size("core")
    chunk = tokens // (nyhi * ncore)
    part = part.reshape(nyhi, ncore, chunk, -1).transpose(1, 0, 2, 3)
    part = lax.all_to_all(part, "core", 0, 0, tiled=True)
    part = jnp.sum(part.astype(jnp.float32), axis=0).astype(jnp.bfloat16)
    part = lax.all_to_all(part, "yhi", 0, 0, tiled=True)
    mixed = jnp.sum(part.astype(jnp.float32), axis=0).astype(jnp.bfloat16)
    return (mixed, key_flat, value_flat)


def solution(mesh):
    devices = mesh.devices
    nseq, nten = devices.shape
    nz = len({d.coords[2] for d in devices[:, 0]})
    nx = len({d.coords[0] for d in devices[:, 0]})
    ncore = len({d.core_on_chip for d in devices[0, :]})
    split = Mesh(devices.reshape(nz, nx, nseq // (nz * nx), nten // ncore, ncore), SEQ + TEN)
    seq, ten = SEQ, TEN
    placed = (
        P(seq, ten),
        P(),
        P(None, ten),
        P(None, ten),
        P(None, ten),
        P(ten, None),
        P(),
        P(),
        P(),
    )
    return jax.shard_map(
        on_device,
        mesh=split,
        in_specs=placed,
        out_specs=(P(seq + ten, None), P(seq, ten), P(seq, ten)),
        check_vma=False,
    )
```

```python
import math

import jax
import jax.numpy as jnp
from jax import lax
from jax.sharding import Mesh
from jax.sharding import PartitionSpec as P

rope_base = 1000000.0
norm_eps = 1e-06
masked = -1e30
max_len = 6144

SEQ = ("z", "x", "ylo")
TEN = ("yhi", "core")


def prompt_starts(lengths, token_pos):
    ends = jnp.cumsum(lengths)
    starts = ends - lengths
    before = (ends[None, :] <= token_pos[:, None]).astype(jnp.int32)
    segment = jnp.sum(before, axis=1)
    onehot = segment[:, None] == jnp.arange(lengths.shape[0], dtype=jnp.int32)[None, :]
    return jnp.sum(jnp.where(onehot, starts[None, :], 0), axis=1)


def head_norm_rope(values, gain, rel_pos):
    width = values.shape[-1]
    half = width // 2
    mean_sq = jnp.mean(values * values, axis=-1, keepdims=True)
    normed = values * lax.rsqrt(mean_sq + norm_eps) * gain
    freq = rope_base ** (-jnp.arange(half, dtype=jnp.float32) * 2.0 / width)
    angle = rel_pos.astype(jnp.float32)[:, None] * freq[None, :]
    cosine = jnp.cos(angle)[:, None, :]
    sine = jnp.sin(angle)[:, None, :]
    first = normed[..., :half]
    second = normed[..., half:]
    return jnp.concatenate(
        [first * cosine - second * sine, second * cosine + first * sine], axis=-1
    )


def ring_pairs(n, k, forward, needed):
    out = []
    for src in range(n):
        if forward:
            start, dst = (src - (k - 1)) % n, (src + 1) % n
            reach = [(start + j) % n for j in range(k, n // 2 + 1)]
        else:
            start, dst = (src + (k - 1)) % n, (src - 1) % n
            reach = [(start - j) % n for j in range(k, n // 2 + 1)]
        if any(needed(start, d) for d in reach):
            out.append((src, dst))
    return out


def ring_gather(piece, inner, name, stride, needed=lambda p, d: True):
    n = lax.axis_size(name)
    c = lax.axis_index(name)
    pieces, ids = [piece], [c * stride + inner]
    a = b = piece
    if n % 2 == 0 and n >= 4:
        last = n // 2 - 1
        m = piece.shape[0]
        half = m // 2 if m % 2 == 0 else m
        for s in range(1, last + 1):
            if s == last:
                far = ((c + n // 2) % n) * stride
                ahead = [(src, (src + 2) % n) for src in range(n) if needed((src - (last - 1)) % n, (src + 2) % n)]
                pieces.append(lax.ppermute(a[:half], name, ahead))
                ids.append(far + inner[:half])
                if half < m:
                    behind = [(src, (src - 2) % n) for src in range(n) if needed((src + (last - 1)) % n, (src - 2) % n)]
                    pieces.append(lax.ppermute(b[half:], name, behind))
                    ids.append(far + inner[half:])
            a = lax.ppermute(a, name, ring_pairs(n, s, True, needed))
            b = lax.ppermute(b, name, ring_pairs(n, s, False, needed))
            pieces += [a, b]
            ids += [((c - s) % n) * stride + inner, ((c + s) % n) * stride + inner]
        return jnp.concatenate(pieces, axis=0), jnp.concatenate(ids, axis=0)
    for s in range(1, (n - 1) // 2 + 1):
        a = lax.ppermute(a, name, ring_pairs(n, s, True, needed))
        b = lax.ppermute(b, name, ring_pairs(n, s, False, needed))
        pieces += [a, b]
        ids += [((c - s) % n) * stride + inner, ((c + s) % n) * stride + inner]
    if n % 2 == 0:
        s = n // 2
        far = ((c + s) % n) * stride
        m = piece.shape[0]
        if m % 2 == 0:
            pieces += [
                lax.ppermute(a[: m // 2], name, ring_pairs(n, s, True, needed)),
                lax.ppermute(b[m // 2 :], name, ring_pairs(n, s, False, needed)),
            ]
            ids += [far + inner[: m // 2], far + inner[m // 2 :]]
        else:
            pieces += [lax.ppermute(a, name, ring_pairs(n, s, True, needed))]
            ids += [far + inner]
    return jnp.concatenate(pieces, axis=0), jnp.concatenate(ids, axis=0)


def on_device(hidden_in, norm_gain, w_query, w_key, w_value, w_out, q_gain, k_gain, lengths):
    tokens = hidden_in.shape[0]
    width = w_query.shape[0]
    head_dim = q_gain.shape[0]
    q_cols = w_query.shape[1]
    kv_cols = w_key.shape[1]
    kv_local = kv_cols // head_dim
    group = q_cols // kv_cols
    combined = jnp.concatenate([w_query, w_key, w_value], axis=1)
    piece = lax.all_gather(hidden_in, TEN, axis=1, tiled=True)
    wide = piece.astype(jnp.float32)
    scaled = (wide * norm_gain[None, :]).astype(jnp.bfloat16)
    acc = jnp.dot(scaled, combined, preferred_element_type=jnp.float32)
    sumsq = jnp.sum(wide * wide, axis=1)
    proj = acc * lax.rsqrt(sumsq / width + norm_eps)[:, None]
    block_index = lax.axis_index(SEQ)
    token_pos = block_index * tokens + jnp.arange(tokens, dtype=jnp.int32)
    seg_start = prompt_starts(lengths, token_pos)
    rel_pos = token_pos - seg_start
    queries = head_norm_rope(
        proj[:, :q_cols].reshape(tokens, kv_local * group, head_dim), q_gain, rel_pos
    ).astype(jnp.bfloat16)
    keys = head_norm_rope(
        proj[:, q_cols : q_cols + kv_cols].reshape(tokens, kv_local, head_dim), k_gain, rel_pos
    ).astype(jnp.bfloat16)
    key_flat = keys.reshape(tokens, kv_cols)
    value_flat = proj[:, q_cols + kv_cols :].astype(jnp.bfloat16)

    nx, nlo = lax.axis_size("x"), lax.axis_size("ylo")
    piece = jnp.concatenate([key_flat, value_flat], axis=1)[None]
    block_ids = jnp.zeros((1,), jnp.int32)
    plane = nx * nlo
    piece = lax.all_to_all(jnp.broadcast_to(piece, (plane,) + piece.shape[1:]), ("x", "ylo"), 0, 0, tiled=True)
    block_ids = jnp.arange(plane, dtype=jnp.int32)
    back = -(-(-(-(max_len - 1) // tokens)) // plane)
    piece, block_ids = ring_gather(piece, block_ids, "z", plane, lambda p, d: 1 <= d - p <= back)
    span = piece.shape[0] * tokens
    kv_all = piece.reshape(span, 2 * kv_cols)
    key_pos = (block_ids[:, None] * tokens + jnp.arange(tokens, dtype=jnp.int32)[None, :]).reshape(span)
    key_heads = kv_all[:, :kv_cols].reshape(span, kv_local, head_dim)
    value_heads = kv_all[:, kv_cols:].reshape(span, kv_local, head_dim)
    query_grid = queries.reshape(tokens, kv_local, group, head_dim)
    inv_root = 1.0 / math.sqrt(head_dim)
    score = (
        jnp.einsum("qhgd,khd->hgqk", query_grid, key_heads, preferred_element_type=jnp.float32)
        * inv_root
    )
    visible = (key_pos[None, :] >= seg_start[:, None]) & (key_pos[None, :] <= token_pos[:, None])
    score = jnp.where(visible[None, None], score, masked)
    top = jnp.max(score, axis=-1, keepdims=True)
    weights = jnp.where(visible[None, None], jnp.exp(score - top), 0.0)
    denom = jnp.sum(weights, axis=-1)
    summed = jnp.einsum(
        "hgqk,khd->hgqd",
        weights.astype(jnp.bfloat16),
        value_heads,
        preferred_element_type=jnp.float32,
    )
    attn = summed / denom[..., None]
    attn = jnp.transpose(attn, (2, 0, 1, 3)).reshape(tokens, q_cols).astype(jnp.bfloat16)
    part = jnp.dot(attn, w_out, preferred_element_type=jnp.float32).astype(jnp.bfloat16)
    nyhi = lax.axis_size("yhi")
    ncore = lax.axis_size("core")
    chunk = tokens // (nyhi * ncore)
    part = part.reshape(nyhi, ncore, chunk, -1).transpose(1, 0, 2, 3)
    part = lax.all_to_all(part, "core", 0, 0, tiled=True)
    part = jnp.sum(part.astype(jnp.float32), axis=0).astype(jnp.bfloat16)
    part = lax.all_to_all(part, "yhi", 0, 0, tiled=True)
    mixed = jnp.sum(part.astype(jnp.float32), axis=0).astype(jnp.bfloat16)
    return (mixed, key_flat, value_flat)


def solution(mesh):
    devices = mesh.devices
    nseq, nten = devices.shape
    nz = len({d.coords[2] for d in devices[:, 0]})
    nx = len({d.coords[0] for d in devices[:, 0]})
    ncore = len({d.core_on_chip for d in devices[0, :]})
    split = Mesh(devices.reshape(nz, nx, nseq // (nz * nx), nten // ncore, ncore), SEQ + TEN)
    seq, ten = SEQ, TEN
    placed = (
        P(seq, ten),
        P(),
        P(None, ten),
        P(None, ten),
        P(None, ten),
        P(ten, None),
        P(),
        P(),
        P(),
    )
    return jax.shard_map(
        on_device,
        mesh=split,
        in_specs=placed,
        out_specs=(P(seq + ten, None), P(seq, ten), P(seq, ten)),
        check_vma=False,
    )
```
